768 devices in a mesh: tiles: 96 (over x, z, core), cams: 8 (over y).
Axes of the slice: x: 4, y: 8, z: 12, core: 2. Of those that a mesh axis runs over, the one named last changes fastest.
Arguments:
- offsets: float32 [2, 196608], P(None, ('tiles', 'cams')), may hold values from -6 to 6
- factor_diag: float32 [2, 196608], P(None, ('tiles', 'cams')), may hold values from 0.8 to 4
- factor_off: float32 [196608], P(('tiles', 'cams')), may hold values from -4 to 4
- logit: float32 [196608], P(('tiles', 'cams')), may hold values from -6 to 6
- appearance: float32 [19, 196608], P(None, ('tiles', 'cams')), may hold values from -6 to 6
- cam_linear: float32 [8, 4], P('cams'), may hold values from -0.3 to 0.3
- cam_shift: float32 [8, 2], P('cams'), may hold values from -2 to 2
- block_lists: int32 [8, 1536, 2, 3], P('cams', 'tiles'), may hold values from 0 to 24575, as said below
- pix_grad: bfloat16 [19, 8, 393216], P(None, 'cams', 'tiles'), may hold values from -6 to 6
Outputs:
- rendered: float32 [19, 8, 393216], P(None, 'cams', 'tiles')
- grad_geometry: float32 [6, 196608], P(None, ('tiles', 'cams'))
- grad_appearance: float32 [19, 196608], P(None, ('tiles', 'cams'))
The draws below stay inside these ranges and needn't reach their ends.
Inputs may be any that keep to these rules, and one draw needn't show every extreme that they name: `block_lists`: call blocks k * 256 to (k+1) * 256 - 1 column k. For each camera and each aligned run of 16 tiles (the tiles of one device), at most 2 list entries of both slabs together name blocks of one column, and exactly 2 name blocks of some column.
All inputs are finite; a program needn't handle non-finite values.
Results may differ from the reference program's by a relative error of at most 0.012.
The reference program's roundings to bfloat16 on the way count: a program that leaves them out, or rounds other values in their place, can miss the bound.
Values may be sent and summed in bfloat16 or wider, within the bound.
No kernel may reach another device: no remote copies, remote signals or barrier semaphores. Data moves between devices by JAX's collectives and lax.ppermute only.
A program may use at most 32 MiB of HBM per device.

```python
import math
import jax
import jax.numpy as jnp
from jax import lax

SIDE = 16
TPD = 16
LIST = 3
BLK = 8
FEAT = 19
CAMS = 8
COLUMNS = 96
ITILES = 1536
PIX = 256
CAP = 2
COLBLK = 256
NG = 196608


def draw_block_lists(key, part):
    key_full, key_score, key_order, key_block = jax.random.split(key, 4)
    slot_total = COLUMNS * CAP
    entry_total = 2 * TPD * LIST
    slot_ids = jnp.arange(slot_total, dtype=jnp.int32)
    slot_column = slot_ids // CAP
    filled = jax.random.randint(key_full, (CAMS, COLUMNS, 1), 0, COLUMNS)
    score = jax.random.randint(key_score, (CAMS, COLUMNS, slot_total), 0, 2 ** 20) * slot_total + slot_ids
    score = jnp.where(slot_column[None, None, :] == filled, slot_ids - slot_total - 1, score)
    chosen = jnp.argsort(score, axis=-1, stable=True)[..., :entry_total]
    entry_ids = jnp.arange(entry_total, dtype=jnp.int32)
    mixing = jax.random.randint(key_order, (CAMS, COLUMNS, entry_total), 0, 2 ** 20) * entry_total + entry_ids
    order = jnp.argsort(mixing, axis=-1, stable=True)
    slots = jnp.take_along_axis(chosen, order, axis=-1)
    column = slots // CAP
    in_column = jax.random.randint(key_block, (CAMS, COLUMNS, entry_total), 0, COLBLK)
    block_ids = column * COLBLK + in_column
    return block_ids.reshape(CAMS, ITILES, 2, LIST).astype(jnp.int32)


def levels(key, shape, cuts, low, high):
    def one(dim, parts):
        draws = jax.random.uniform(jax.random.fold_in(jax.random.fold_in(key, 6), dim), (parts,), jnp.float32, low / len(cuts), high / len(cuts))
        return jnp.repeat(jnp.exp(draws), shape[dim] // parts).reshape((-1,) + (1,) * (len(shape) - dim - 1))

    loudness = one(*cuts[0])
    for cut in cuts[1:]:
        loudness = loudness * one(*cut)
    return loudness


def scatter_about(stream_key, dims, width, bound, shards=(), held_as=jnp.bfloat16):
    array = jax.random.normal(stream_key, dims, jnp.float32) * width
    if len(shards) > 0:
        array = levels(stream_key, dims, shards, -0.22, 0.18) * array
    return jnp.clip(array, min=-bound, max=bound).astype(held_as)


def setup_inputs(seed: int = 0) -> dict:
    streams_of = jax.random.split(jax.random.key(seed), 10)
    offsets = jnp.clip(jax.random.uniform(streams_of[0], (2, NG), jnp.float32, -6.0, 6.0) * levels(streams_of[0], (2, NG), ((1, 768),), -0.4, 0.0), -6.0, 6.0)
    factor_diag = jnp.clip(jnp.exp(math.log(4.0) - 1.609438 * jax.random.uniform(streams_of[1], (2, NG), jnp.float32) ** levels(streams_of[1], (2, NG), ((1, 768),), -0.2, 0.2)), 0.8, 4.0)
    factor_off = scatter_about(streams_of[2], (NG,), 1.0, 4.0, ((0, 768),), jnp.float32)
    logit = scatter_about(streams_of[3], (NG,), 1.5, 6.0, ((0, 768),), jnp.float32)
    appearance = scatter_about(streams_of[4], (FEAT, NG), 1.0, 6.0, ((1, 768),), jnp.float32)
    cam_linear = jnp.clip(jax.random.uniform(streams_of[5], (CAMS, 4), jnp.float32, -0.3, 0.3) * levels(streams_of[5], (CAMS, 4), ((0, 8),), -0.4, 0.0), -0.3, 0.3)
    cam_shift = jnp.clip(jax.random.uniform(streams_of[6], (CAMS, 2), jnp.float32, -2.0, 2.0) * levels(streams_of[6], (CAMS, 2), ((0, 8),), -0.4, 0.0), -2.0, 2.0)
    block_lists = draw_block_lists(jax.random.fold_in(streams_of[9], 71), 0)
    pix_grad = scatter_about(streams_of[8], (FEAT, CAMS, ITILES * PIX), 1.0, 6.0, ((1, 8), (2, 96)))
    return dict(offsets=offsets, factor_diag=factor_diag, factor_off=factor_off, logit=logit, appearance=appearance, cam_linear=cam_linear, cam_shift=cam_shift, block_lists=block_lists, pix_grad=pix_grad)


def to_half(values):
    rounded = lax.optimization_barrier(values.astype(jnp.bfloat16))
    return rounded.astype(jnp.float32)

def project(geometry, linear, camera_shift):
    lin_xx = 1.0 + linear[0]
    lin_xy = linear[1]
    lin_yx = linear[2]
    lin_yy = 1.0 + linear[3]
    diag_x = geometry[2]
    diag_y = geometry[3]
    lower = geometry[4]
    cov_xx = diag_x * diag_x
    cov_xy = diag_x * lower
    cov_yy = lower * lower + diag_y * diag_y
    half_xx = lin_xx * cov_xx + lin_xy * cov_xy
    half_xy = lin_xx * cov_xy + lin_xy * cov_yy
    half_yx = lin_yx * cov_xx + lin_yy * cov_xy
    half_yy = lin_yx * cov_xy + lin_yy * cov_yy
    img_xx = half_xx * lin_xx + half_xy * lin_xy + 0.3
    img_xy = half_xx * lin_yx + half_xy * lin_yy
    img_yy = half_yx * lin_yx + half_yy * lin_yy + 0.3
    determ = img_xx * img_yy - img_xy * img_xy
    centre_x = lin_xx * geometry[0] + lin_xy * geometry[1] + camera_shift[0]
    centre_y = lin_yx * geometry[0] + lin_yy * geometry[1] + camera_shift[1]
    opacity = 0.95 * jax.nn.sigmoid(geometry[5])
    return jnp.stack([centre_x, centre_y, img_yy / determ, -img_xy / determ, img_xx / determ, opacity])

def render_tile(projected, colours):
    pixels = jnp.arange(SIDE * SIDE)
    across = (pixels % SIDE).astype(jnp.float32) + 0.5 - SIDE / 2
    downward = (pixels // SIDE).astype(jnp.float32) + 0.5 - SIDE / 2
    delta_x = across[None, :] - projected[0][:, None]
    delta_y = downward[None, :] - projected[1][:, None]
    quadric = projected[2][:, None] * delta_x * delta_x + 2.0 * projected[3][:, None] * delta_x * delta_y + projected[4][:, None] * delta_y * delta_y
    coverage = projected[5][:, None] * jnp.exp(-0.5 * quadric)
    log_keep = jnp.log1p(-coverage)
    weight = jnp.exp(jnp.cumsum(log_keep, axis=0) - log_keep) * coverage
    return jnp.dot(colours, weight, precision=lax.Precision.HIGHEST, preferred_element_type=jnp.float32)

def tile_grads(projected, colours, cotangent):
    per_tile = projected.shape[1] // TPD
    channels = colours.shape[0]
    proj_tiles = projected.reshape(6, TPD, per_tile)
    colour_tiles = colours.reshape(channels, TPD, per_tile)

    def forward(proj_arg, colour_arg):
        return jax.vmap(render_tile, in_axes=(1, 1), out_axes=1)(proj_arg, colour_arg)
    picture, pullback = jax.vjp(forward, proj_tiles, colour_tiles)
    grad_proj, grad_colour = pullback(cotangent)
    return (picture, grad_proj.reshape(6, -1), grad_colour.reshape(channels, -1))

def reference(offsets, factor_diag, factor_off, logit, appearance, cam_linear, cam_shift, block_lists, pix_grad):
    geometry = jnp.concatenate([offsets, factor_diag, factor_off[None, :], logit[None, :]], axis=0)
    channels = appearance.shape[0]
    gaussians = geometry.shape[1]
    within = jnp.arange(BLK, dtype=jnp.int32)

    def visit(totals, position):
        grad_geometry, grad_appearance = totals
        camera = position // COLUMNS
        column = position % COLUMNS
        entries = lax.dynamic_slice(block_lists, (camera, column * TPD, jnp.int32(0), jnp.int32(0)), (1, TPD, 2, LIST)).reshape(-1)
        gauss_index = (entries[:, None] * BLK + within[None, :]).reshape(-1)
        raw_params = geometry[:, gauss_index]
        colours = to_half(appearance[:, gauss_index])
        linear = cam_linear[camera]
        camera_shift = cam_shift[camera]
        projected = to_half(project(raw_params, linear, camera_shift))
        cotangent = lax.dynamic_slice(pix_grad, (jnp.int32(0), camera, column * TPD * PIX), (channels, 1, TPD * PIX))
        cotangent = cotangent.reshape(channels, TPD, PIX).astype(jnp.float32)
        picture, grad_proj, grad_colour = tile_grads(projected, colours, cotangent)
        grad_proj = to_half(grad_proj)
        grad_colour = to_half(grad_colour)
        unused, pull_params = jax.vjp(lambda params: project(params, linear, camera_shift), raw_params)
        grad_raw = pull_params(grad_proj)[0]
        grad_geometry = grad_geometry.at[:, gauss_index].add(grad_raw)
        grad_appearance = grad_appearance.at[:, gauss_index].add(grad_colour)
        return ((grad_geometry, grad_appearance), picture.reshape(channels, TPD * PIX))
    initial = (jnp.zeros((6, gaussians), jnp.float32), jnp.zeros((channels, gaussians), jnp.float32))
    totals, pictures = lax.scan(visit, initial, jnp.arange(CAMS * COLUMNS, dtype=jnp.int32))
    rendered = pictures.reshape(CAMS, COLUMNS, channels, TPD * PIX).transpose(2, 0, 1, 3).reshape(channels, CAMS, ITILES * PIX)
    return (rendered, totals[0], totals[1])
```

```python
import jax
import jax.numpy as jnp
from jax import lax
from jax.sharding import PartitionSpec as P

SIDE = 16
TPD = 16
LIST = 3
BLK = 8


def project(geometry, linear, camera_shift):
    lin_xx = 1.0 + linear[0]
    lin_xy = linear[1]
    lin_yx = linear[2]
    lin_yy = 1.0 + linear[3]
    diag_x = geometry[2]
    diag_y = geometry[3]
    lower = geometry[4]
    cov_xx = diag_x * diag_x
    cov_xy = diag_x * lower
    cov_yy = lower * lower + diag_y * diag_y
    half_xx = lin_xx * cov_xx + lin_xy * cov_xy
    half_xy = lin_xx * cov_xy + lin_xy * cov_yy
    half_yx = lin_yx * cov_xx + lin_yy * cov_xy
    half_yy = lin_yx * cov_xy + lin_yy * cov_yy
    img_xx = half_xx * lin_xx + half_xy * lin_xy + 0.3
    img_xy = half_xx * lin_yx + half_xy * lin_yy
    img_yy = half_yx * lin_yx + half_yy * lin_yy + 0.3
    determ = img_xx * img_yy - img_xy * img_xy
    centre_x = lin_xx * geometry[0] + lin_xy * geometry[1] + camera_shift[0]
    centre_y = lin_yx * geometry[0] + lin_yy * geometry[1] + camera_shift[1]
    opacity = 0.95 * jax.nn.sigmoid(geometry[5])
    return jnp.stack(
        [centre_x, centre_y, img_yy / determ, -img_xy / determ, img_xx / determ, opacity]
    )


def render_tile(projected, colours):
    pixels = jnp.arange(SIDE * SIDE)
    across = (pixels % SIDE).astype(jnp.float32) + 0.5 - SIDE / 2
    downward = (pixels // SIDE).astype(jnp.float32) + 0.5 - SIDE / 2
    delta_x = across[None, :] - projected[0][:, None]
    delta_y = downward[None, :] - projected[1][:, None]
    quadric = (
        projected[2][:, None] * delta_x * delta_x
        + 2.0 * projected[3][:, None] * delta_x * delta_y
        + projected[4][:, None] * delta_y * delta_y
    )
    coverage = projected[5][:, None] * jnp.exp(-0.5 * quadric)
    log_keep = jnp.log1p(-coverage)
    weight = jnp.exp(jnp.cumsum(log_keep, axis=0) - log_keep) * coverage
    return jnp.dot(
        colours, weight, precision=lax.Precision.HIGHEST, preferred_element_type=jnp.float32
    )


def tile_grads(projected, colours, cotangent):
    per_tile = projected.shape[1] // TPD
    channels = colours.shape[0]
    proj_tiles = projected.reshape(6, TPD, per_tile)
    colour_tiles = colours.reshape(channels, TPD, per_tile)

    def forward(proj_arg, colour_arg):
        return jax.vmap(render_tile, in_axes=(1, 1), out_axes=1)(proj_arg, colour_arg)

    picture, pullback = jax.vjp(forward, proj_tiles, colour_tiles)
    grad_proj, grad_colour = pullback(cotangent)
    return (picture, grad_proj.reshape(6, -1), grad_colour.reshape(channels, -1))


def slot_ranks(entries, blocks_per_column, columns):
    column = entries // blocks_per_column
    in_column = entries % blocks_per_column
    matches = (column[..., None] == jnp.arange(columns, dtype=jnp.int32)).astype(jnp.int32)
    before = jnp.cumsum(matches, axis=-2) - matches
    ranking = jnp.sum(before * matches, axis=-1)
    return (column, ranking, in_column)


def local(
    offsets,
    factor_diag,
    factor_off,
    logit,
    appearance,
    cam_linear,
    cam_shift,
    block_lists,
    pix_grad,
):
    columns = lax.axis_size("tiles")
    capacity = 4 * TPD * LIST // columns
    slot_count = columns * capacity
    channels = appearance.shape[0]
    geometry = jnp.concatenate([offsets, factor_diag, factor_off[None, :], logit[None, :]], axis=0)
    params = jnp.concatenate([geometry, appearance], axis=0)
    params_col = lax.all_gather(params, "cams", axis=1, tiled=True)
    geometry_col = params_col[:6]
    appearance_col = params_col[6:]
    per_column = geometry_col.shape[1] // BLK
    linear = cam_linear[0]
    camera_shift = cam_shift[0]
    entries = block_lists.reshape(-1)
    entry_count = entries.shape[0]
    column, ranking, in_column = slot_ranks(entries, per_column, columns)
    entry_slot = column * capacity + ranking
    request = jnp.zeros((slot_count,), jnp.int32).at[entry_slot].set(in_column)
    wanted = lax.all_to_all(request, "tiles", split_axis=0, concat_axis=0, tiled=True)
    raw_params = geometry_col.reshape(6, per_column, BLK)[:, wanted].reshape(6, slot_count * BLK)
    raw_colours = appearance_col.reshape(channels, per_column, BLK)[:, wanted].reshape(
        channels, slot_count * BLK
    )
    send_proj = project(raw_params, linear, camera_shift).astype(jnp.bfloat16)
    sent = lax.all_to_all(
        jnp.concatenate([send_proj, raw_colours.astype(jnp.bfloat16)], axis=0),
        "tiles",
        split_axis=1,
        concat_axis=1,
        tiled=True,
    )
    got_proj = sent[:6]
    got_colour = sent[6:]
    projected = (
        got_proj.reshape(6, slot_count, BLK)[:, entry_slot]
        .reshape(6, entry_count * BLK)
        .astype(jnp.float32)
    )
    colours = (
        got_colour.reshape(channels, slot_count, BLK)[:, entry_slot]
        .reshape(channels, entry_count * BLK)
        .astype(jnp.float32)
    )
    cotangent = pix_grad.reshape(channels, TPD, -1).astype(jnp.float32)
    picture, grad_proj, grad_colour = tile_grads(projected, colours, cotangent)
    back_proj = (
        jnp.zeros((6, slot_count, BLK), jnp.bfloat16)
        .at[:, entry_slot]
        .set(grad_proj.reshape(6, entry_count, BLK).astype(jnp.bfloat16))
    )
    back_colour = (
        jnp.zeros((channels, slot_count, BLK), jnp.bfloat16)
        .at[:, entry_slot]
        .set(grad_colour.reshape(channels, entry_count, BLK).astype(jnp.bfloat16))
    )
    returned = lax.all_to_all(
        jnp.concatenate([back_proj.reshape(6, -1), back_colour.reshape(channels, -1)], axis=0),
        "tiles",
        split_axis=1,
        concat_axis=1,
        tiled=True,
    )
    ret_proj = returned[:6]
    ret_colour = returned[6:]
    unused, pull_params = jax.vjp(lambda params: project(params, linear, camera_shift), raw_params)
    grad_raw = pull_params(ret_proj.astype(jnp.float32))[0]
    owner_hot = (wanted[:, None] == jnp.arange(per_column, dtype=jnp.int32)[None, :]).astype(
        jnp.float32
    )

    def collect(values, row_count):
        summed = jnp.einsum(
            "rsb,sk->rkb",
            values.reshape(row_count, slot_count, BLK),
            owner_hot,
            precision=lax.Precision.HIGHEST,
        )
        return summed.reshape(row_count, per_column * BLK)

    column_geometry = collect(grad_raw, 6)
    column_colour = collect(ret_colour.astype(jnp.float32), channels)
    grads = lax.psum_scatter(
        jnp.concatenate([column_geometry, column_colour], axis=0),
        "cams",
        scatter_dimension=1,
        tiled=True,
    )
    grad_geometry = grads[:6]
    grad_appearance = grads[6:]
    return (picture.reshape(channels, 1, -1), grad_geometry, grad_appearance)


def solution(mesh):
    return jax.shard_map(
        local,
        mesh=mesh,
        in_specs=(
            P(None, ("tiles", "cams")),
            P(None, ("tiles", "cams")),
            P(("tiles", "cams")),
            P(("tiles", "cams")),
            P(None, ("tiles", "cams")),
            P("cams", None),
            P("cams", None),
            P("cams", "tiles", None, None),
            P(None, "cams", "tiles"),
        ),
        out_specs=(
            P(None, "cams", "tiles"),
            P(None, ("tiles", "cams")),
            P(None, ("tiles", "cams")),
        ),
        check_vma=False,
    )
```

```python
import jax
import jax.numpy as jnp
from jax import lax
from jax.sharding import PartitionSpec as P

SIDE = 16
TPD = 16
LIST = 3
BLK = 8


def project(geometry, linear, camera_shift):
    lin_xx = 1.0 + linear[0]
    lin_xy = linear[1]
    lin_yx = linear[2]
    lin_yy = 1.0 + linear[3]
    diag_x = geometry[2]
    diag_y = geometry[3]
    lower = geometry[4]
    cov_xx = diag_x * diag_x
    cov_xy = diag_x * lower
    cov_yy = lower * lower + diag_y * diag_y
    half_xx = lin_xx * cov_xx + lin_xy * cov_xy
    half_xy = lin_xx * cov_xy + lin_xy * cov_yy
    half_yx = lin_yx * cov_xx + lin_yy * cov_xy
    half_yy = lin_yx * cov_xy + lin_yy * cov_yy
    img_xx = half_xx * lin_xx + half_xy * lin_xy + 0.3
    img_xy = half_xx * lin_yx + half_xy * lin_yy
    img_yy = half_yx * lin_yx + half_yy * lin_yy + 0.3
    determ = img_xx * img_yy - img_xy * img_xy
    centre_x = lin_xx * geometry[0] + lin_xy * geometry[1] + camera_shift[0]
    centre_y = lin_yx * geometry[0] + lin_yy * geometry[1] + camera_shift[1]
    opacity = 0.95 * jax.nn.sigmoid(geometry[5])
    return jnp.stack(
        [centre_x, centre_y, img_yy / determ, -img_xy / determ, img_xx / determ, opacity]
    )


def render_tile(projected, colours):
    pixels = jnp.arange(SIDE * SIDE)
    across = (pixels % SIDE).astype(jnp.float32) + 0.5 - SIDE / 2
    downward = (pixels // SIDE).astype(jnp.float32) + 0.5 - SIDE / 2
    delta_x = across[None, :] - projected[0][:, None]
    delta_y = downward[None, :] - projected[1][:, None]
    quadric = (
        projected[2][:, None] * delta_x * delta_x
        + 2.0 * projected[3][:, None] * delta_x * delta_y
        + projected[4][:, None] * delta_y * delta_y
    )
    coverage = projected[5][:, None] * jnp.exp(-0.5 * quadric)
    log_keep = jnp.log1p(-coverage)
    weight = jnp.exp(jnp.cumsum(log_keep, axis=0) - log_keep) * coverage
    return jnp.dot(
        colours, weight, precision=lax.Precision.HIGHEST, preferred_element_type=jnp.float32
    )


def tile_grads(projected, colours, cotangent):
    per_tile = projected.shape[1] // TPD
    channels = colours.shape[0]
    proj_tiles = projected.reshape(6, TPD, per_tile)
    colour_tiles = colours.reshape(channels, TPD, per_tile)

    def forward(proj_arg, colour_arg):
        return jax.vmap(render_tile, in_axes=(1, 1), out_axes=1)(proj_arg, colour_arg)

    picture, pullback = jax.vjp(forward, proj_tiles, colour_tiles)
    grad_proj, grad_colour = pullback(cotangent)
    return (picture, grad_proj.reshape(6, -1), grad_colour.reshape(channels, -1))


def slot_ranks(entries, blocks_per_column, columns):
    column = entries // blocks_per_column
    in_column = entries % blocks_per_column
    matches = (column[..., None] == jnp.arange(columns, dtype=jnp.int32)).astype(jnp.int32)
    before = jnp.cumsum(matches, axis=-2) - matches
    ranking = jnp.sum(before * matches, axis=-1)
    return (column, ranking, in_column)


def local(
    offsets,
    factor_diag,
    factor_off,
    logit,
    appearance,
    cam_linear,
    cam_shift,
    block_lists,
    pix_grad,
):
    columns = lax.axis_size("tiles")
    capacity = 4 * TPD * LIST // columns
    slot_count = columns * capacity
    channels = appearance.shape[0]
    geometry = jnp.concatenate([offsets, factor_diag, factor_off[None, :], logit[None, :]], axis=0)
    params = jnp.concatenate([geometry, appearance], axis=0)
    cams = lax.axis_size("cams")
    gathered = lax.all_to_all(
        jnp.broadcast_to(params[None], (cams,) + params.shape), "cams", 0, 0, tiled=True
    )
    params_col = gathered.transpose(1, 0, 2).reshape(params.shape[0], cams * params.shape[1])
    geometry_col = params_col[:6]
    appearance_col = params_col[6:]
    per_column = geometry_col.shape[1] // BLK
    linear = cam_linear[0]
    camera_shift = cam_shift[0]
    entries = block_lists.reshape(-1)
    entry_count = entries.shape[0]
    column, ranking, in_column = slot_ranks(entries, per_column, columns)
    entry_slot = column * capacity + ranking
    request = jnp.zeros((slot_count,), jnp.int32).at[entry_slot].set(in_column)
    wanted = lax.all_to_all(request, "tiles", split_axis=0, concat_axis=0, tiled=True)
    raw_params = geometry_col.reshape(6, per_column, BLK)[:, wanted].reshape(6, slot_count * BLK)
    raw_colours = appearance_col.reshape(channels, per_column, BLK)[:, wanted].reshape(
        channels, slot_count * BLK
    )
    send_proj = project(raw_params, linear, camera_shift).astype(jnp.bfloat16)
    sent = lax.all_to_all(
        jnp.concatenate([send_proj, raw_colours.astype(jnp.bfloat16)], axis=0),
        "tiles",
        split_axis=1,
        concat_axis=1,
        tiled=True,
    )
    got_proj = sent[:6]
    got_colour = sent[6:]
    projected = (
        got_proj.reshape(6, slot_count, BLK)[:, entry_slot]
        .reshape(6, entry_count * BLK)
        .astype(jnp.float32)
    )
    colours = (
        got_colour.reshape(channels, slot_count, BLK)[:, entry_slot]
        .reshape(channels, entry_count * BLK)
        .astype(jnp.float32)
    )
    cotangent = pix_grad.reshape(channels, TPD, -1).astype(jnp.float32)
    picture, grad_proj, grad_colour = tile_grads(projected, colours, cotangent)
    back_proj = (
        jnp.zeros((6, slot_count, BLK), jnp.bfloat16)
        .at[:, entry_slot]
        .set(grad_proj.reshape(6, entry_count, BLK).astype(jnp.bfloat16))
    )
    back_colour = (
        jnp.zeros((channels, slot_count, BLK), jnp.bfloat16)
        .at[:, entry_slot]
        .set(grad_colour.reshape(channels, entry_count, BLK).astype(jnp.bfloat16))
    )
    returned = lax.all_to_all(
        jnp.concatenate([back_proj.reshape(6, -1), back_colour.reshape(channels, -1)], axis=0),
        "tiles",
        split_axis=1,
        concat_axis=1,
        tiled=True,
    )
    ret_proj = returned[:6]
    ret_colour = returned[6:]
    unused, pull_params = jax.vjp(lambda params: project(params, linear, camera_shift), raw_params)
    grad_raw = pull_params(ret_proj.astype(jnp.float32))[0]
    owner_hot = (wanted[:, None] == jnp.arange(per_column, dtype=jnp.int32)[None, :]).astype(
        jnp.float32
    )

    def collect(values, row_count):
        summed = jnp.einsum(
            "rsb,sk->rkb",
            values.reshape(row_count, slot_count, BLK),
            owner_hot,
            precision=lax.Precision.HIGHEST,
        )
        return summed.reshape(row_count, per_column * BLK)

    column_geometry = collect(grad_raw, 6)
    column_colour = collect(ret_colour.astype(jnp.float32), channels)
    column_all = jnp.concatenate([column_geometry, column_colour], axis=0)
    rows = column_all.shape[0]
    grads = lax.all_to_all(
        column_all.reshape(rows, cams, -1), "cams", 1, 1, tiled=True
    ).sum(axis=1)
    grad_geometry = grads[:6]
    grad_appearance = grads[6:]
    return (picture.reshape(channels, 1, -1), grad_geometry, grad_appearance)


def solution(mesh):
    return jax.shard_map(
        local,
        mesh=mesh,
        in_specs=(
            P(None, ("tiles", "cams")),
            P(None, ("tiles", "cams")),
            P(("tiles", "cams")),
            P(("tiles", "cams")),
            P(None, ("tiles", "cams")),
            P("cams", None),
            P("cams", None),
            P("cams", "tiles", None, None),
            P(None, "cams", "tiles"),
        ),
        out_specs=(
            P(None, "cams", "tiles"),
            P(None, ("tiles", "cams")),
            P(None, ("tiles", "cams")),
        ),
        check_vma=False,
    )
```

```python
import jax
import jax.numpy as jnp
from jax import lax
from jax.sharding import PartitionSpec as P

SIDE = 16
TPD = 16
LIST = 3
BLK = 8


def project(geometry, linear, camera_shift):
    lin_xx = 1.0 + linear[0]
    lin_xy = linear[1]
    lin_yx = linear[2]
    lin_yy = 1.0 + linear[3]
    diag_x = geometry[2]
    diag_y = geometry[3]
    lower = geometry[4]
    cov_xx = diag_x * diag_x
    cov_xy = diag_x * lower
    cov_yy = lower * lower + diag_y * diag_y
    half_xx = lin_xx * cov_xx + lin_xy * cov_xy
    half_xy = lin_xx * cov_xy + lin_xy * cov_yy
    half_yx = lin_yx * cov_xx + lin_yy * cov_xy
    half_yy = lin_yx * cov_xy + lin_yy * cov_yy
    img_xx = half_xx * lin_xx + half_xy * lin_xy + 0.3
    img_xy = half_xx * lin_yx + half_xy * lin_yy
    img_yy = half_yx * lin_yx + half_yy * lin_yy + 0.3
    determ = img_xx * img_yy - img_xy * img_xy
    centre_x = lin_xx * geometry[0] + lin_xy * geometry[1] + camera_shift[0]
    centre_y = lin_yx * geometry[0] + lin_yy * geometry[1] + camera_shift[1]
    opacity = 0.95 * jax.nn.sigmoid(geometry[5])
    return jnp.stack(
        [centre_x, centre_y, img_yy / determ, -img_xy / determ, img_xx / determ, opacity]
    )


def render_tile(projected, colours):
    pixels = jnp.arange(SIDE * SIDE)
    across = (pixels % SIDE).astype(jnp.float32) + 0.5 - SIDE / 2
    downward = (pixels // SIDE).astype(jnp.float32) + 0.5 - SIDE / 2
    delta_x = across[None, :] - projected[0][:, None]
    delta_y = downward[None, :] - projected[1][:, None]
    quadric = (
        projected[2][:, None] * delta_x * delta_x
        + 2.0 * projected[3][:, None] * delta_x * delta_y
        + projected[4][:, None] * delta_y * delta_y
    )
    coverage = projected[5][:, None] * jnp.exp(-0.5 * quadric)
    log_keep = jnp.log1p(-coverage)
    weight = jnp.exp(jnp.cumsum(log_keep, axis=0) - log_keep) * coverage
    return jnp.dot(
        colours, weight, precision=lax.Precision.HIGHEST, preferred_element_type=jnp.float32
    )


def tile_grads(projected, colours, cotangent):
    per_tile = projected.shape[1] // TPD
    channels = colours.shape[0]
    proj_tiles = projected.reshape(6, TPD, per_tile)
    colour_tiles = colours.reshape(channels, TPD, per_tile)

    def forward(proj_arg, colour_arg):
        return jax.vmap(render_tile, in_axes=(1, 1), out_axes=1)(proj_arg, colour_arg)

    picture, pullback = jax.vjp(forward, proj_tiles, colour_tiles)
    grad_proj, grad_colour = pullback(cotangent)
    return (picture, grad_proj.reshape(6, -1), grad_colour.reshape(channels, -1))


def slot_ranks(entries, blocks_per_column, columns):
    column = entries // blocks_per_column
    in_column = entries % blocks_per_column
    matches = (column[..., None] == jnp.arange(columns, dtype=jnp.int32)).astype(jnp.int32)
    before = jnp.cumsum(matches, axis=-2) - matches
    ranking = jnp.sum(before * matches, axis=-1)
    return (column, ranking, in_column)


def local(
    offsets,
    factor_diag,
    factor_off,
    logit,
    appearance,
    cam_linear,
    cam_shift,
    block_lists,
    pix_grad,
):
    columns = lax.axis_size("tiles")
    capacity = 4 * TPD * LIST // columns
    slot_count = columns * capacity
    channels = appearance.shape[0]
    geometry = jnp.concatenate([offsets, factor_diag, factor_off[None, :], logit[None, :]], axis=0)
    params = jnp.concatenate([geometry, appearance], axis=0)
    cams = lax.axis_size("cams")
    shifted = [params] + [
        lax.ppermute(params, "cams", [(i, (i + s) % cams) for i in range(cams)])
        for s in range(1, cams)
    ]
    source_shift = (lax.axis_index("cams") - jnp.arange(cams)) % cams
    gathered = jnp.take(jnp.stack(shifted), source_shift, axis=0)
    params_col = gathered.transpose(1, 0, 2).reshape(params.shape[0], cams * params.shape[1])
    geometry_col = params_col[:6]
    appearance_col = params_col[6:]
    per_column = geometry_col.shape[1] // BLK
    linear = cam_linear[0]
    camera_shift = cam_shift[0]
    entries = block_lists.reshape(-1)
    entry_count = entries.shape[0]
    column, ranking, in_column = slot_ranks(entries, per_column, columns)
    entry_slot = column * capacity + ranking
    request = jnp.zeros((slot_count,), jnp.int32).at[entry_slot].set(in_column)
    wanted = lax.all_to_all(request, "tiles", split_axis=0, concat_axis=0, tiled=True)
    raw_params = geometry_col.reshape(6, per_column, BLK)[:, wanted].reshape(6, slot_count * BLK)
    raw_colours = appearance_col.reshape(channels, per_column, BLK)[:, wanted].reshape(
        channels, slot_count * BLK
    )
    send_proj = project(raw_params, linear, camera_shift).astype(jnp.bfloat16)
    sent = lax.all_to_all(
        jnp.concatenate([send_proj, raw_colours.astype(jnp.bfloat16)], axis=0),
        "tiles",
        split_axis=1,
        concat_axis=1,
        tiled=True,
    )
    got_proj = sent[:6]
    got_colour = sent[6:]
    projected = (
        got_proj.reshape(6, slot_count, BLK)[:, entry_slot]
        .reshape(6, entry_count * BLK)
        .astype(jnp.float32)
    )
    colours = (
        got_colour.reshape(channels, slot_count, BLK)[:, entry_slot]
        .reshape(channels, entry_count * BLK)
        .astype(jnp.float32)
    )
    cotangent = pix_grad.reshape(channels, TPD, -1).astype(jnp.float32)
    picture, grad_proj, grad_colour = tile_grads(projected, colours, cotangent)
    back_proj = (
        jnp.zeros((6, slot_count, BLK), jnp.bfloat16)
        .at[:, entry_slot]
        .set(grad_proj.reshape(6, entry_count, BLK).astype(jnp.bfloat16))
    )
    back_colour = (
        jnp.zeros((channels, slot_count, BLK), jnp.bfloat16)
        .at[:, entry_slot]
        .set(grad_colour.reshape(channels, entry_count, BLK).astype(jnp.bfloat16))
    )
    returned = lax.all_to_all(
        jnp.concatenate([back_proj.reshape(6, -1), back_colour.reshape(channels, -1)], axis=0),
        "tiles",
        split_axis=1,
        concat_axis=1,
        tiled=True,
    )
    ret_proj = returned[:6]
    ret_colour = returned[6:]
    unused, pull_params = jax.vjp(lambda params: project(params, linear, camera_shift), raw_params)
    grad_raw = pull_params(ret_proj.astype(jnp.float32))[0]
    owner_hot = (wanted[:, None] == jnp.arange(per_column, dtype=jnp.int32)[None, :]).astype(
        jnp.float32
    )

    def collect(values, row_count):
        summed = jnp.einsum(
            "rsb,sk->rkb",
            values.reshape(row_count, slot_count, BLK),
            owner_hot,
            precision=lax.Precision.HIGHEST,
        )
        return summed.reshape(row_count, per_column * BLK)

    column_geometry = collect(grad_raw, 6)
    column_colour = collect(ret_colour.astype(jnp.float32), channels)
    column_all = jnp.concatenate([column_geometry, column_colour], axis=0)
    rows = column_all.shape[0]
    grads = lax.all_to_all(
        column_all.reshape(rows, cams, -1), "cams", 1, 1, tiled=True
    ).sum(axis=1)
    grad_geometry = grads[:6]
    grad_appearance = grads[6:]
    return (picture.reshape(channels, 1, -1), grad_geometry, grad_appearance)


def solution(mesh):
    return jax.shard_map(
        local,
        mesh=mesh,
        in_specs=(
            P(None, ("tiles", "cams")),
            P(None, ("tiles", "cams")),
            P(("tiles", "cams")),
            P(("tiles", "cams")),
            P(None, ("tiles", "cams")),
            P("cams", None),
            P("cams", None),
            P("cams", "tiles", None, None),
            P(None, "cams", "tiles"),
        ),
        out_specs=(
            P(None, "cams", "tiles"),
            P(None, ("tiles", "cams")),
            P(None, ("tiles", "cams")),
        ),
        check_vma=False,
    )
```

```python
import jax
import jax.numpy as jnp
from jax import lax
from jax.sharding import PartitionSpec as P

SIDE = 16
TPD = 16
LIST = 3
BLK = 8


def project(geometry, linear, camera_shift):
    lin_xx = 1.0 + linear[0]
    lin_xy = linear[1]
    lin_yx = linear[2]
    lin_yy = 1.0 + linear[3]
    diag_x = geometry[2]
    diag_y = geometry[3]
    lower = geometry[4]
    cov_xx = diag_x * diag_x
    cov_xy = diag_x * lower
    cov_yy = lower * lower + diag_y * diag_y
    half_xx = lin_xx * cov_xx + lin_xy * cov_xy
    half_xy = lin_xx * cov_xy + lin_xy * cov_yy
    half_yx = lin_yx * cov_xx + lin_yy * cov_xy
    half_yy = lin_yx * cov_xy + lin_yy * cov_yy
    img_xx = half_xx * lin_xx + half_xy * lin_xy + 0.3
    img_xy = half_xx * lin_yx + half_xy * lin_yy
    img_yy = half_yx * lin_yx + half_yy * lin_yy + 0.3
    determ = img_xx * img_yy - img_xy * img_xy
    centre_x = lin_xx * geometry[0] + lin_xy * geometry[1] + camera_shift[0]
    centre_y = lin_yx * geometry[0] + lin_yy * geometry[1] + camera_shift[1]
    opacity = 0.95 * jax.nn.sigmoid(geometry[5])
    return jnp.stack(
        [centre_x, centre_y, img_yy / determ, -img_xy / determ, img_xx / determ, opacity]
    )


def render_tile(projected, colours):
    pixels = jnp.arange(SIDE * SIDE)
    across = (pixels % SIDE).astype(jnp.float32) + 0.5 - SIDE / 2
    downward = (pixels // SIDE).astype(jnp.float32) + 0.5 - SIDE / 2
    delta_x = across[None, :] - projected[0][:, None]
    delta_y = downward[None, :] - projected[1][:, None]
    quadric = (
        projected[2][:, None] * delta_x * delta_x
        + 2.0 * projected[3][:, None] * delta_x * delta_y
        + projected[4][:, None] * delta_y * delta_y
    )
    coverage = projected[5][:, None] * jnp.exp(-0.5 * quadric)
    log_keep = jnp.log1p(-coverage)
    weight = jnp.exp(jnp.cumsum(log_keep, axis=0) - log_keep) * coverage
    return jnp.dot(
        colours, weight, precision=lax.Precision.HIGHEST, preferred_element_type=jnp.float32
    )


def tile_grads(projected, colours, cotangent):
    per_tile = projected.shape[1] // TPD
    channels = colours.shape[0]
    proj_tiles = projected.reshape(6, TPD, per_tile)
    colour_tiles = colours.reshape(channels, TPD, per_tile)

    def forward(proj_arg, colour_arg):
        return jax.vmap(render_tile, in_axes=(1, 1), out_axes=1)(proj_arg, colour_arg)

    picture, pullback = jax.vjp(forward, proj_tiles, colour_tiles)
    grad_proj, grad_colour = pullback(cotangent)
    return (picture, grad_proj.reshape(6, -1), grad_colour.reshape(channels, -1))


def slot_ranks(entries, blocks_per_column, columns):
    column = entries // blocks_per_column
    in_column = entries % blocks_per_column
    matches = (column[..., None] == jnp.arange(columns, dtype=jnp.int32)).astype(jnp.int32)
    before = jnp.cumsum(matches, axis=-2) - matches
    ranking = jnp.sum(before * matches, axis=-1)
    return (column, ranking, in_column)


def local(
    offsets,
    factor_diag,
    factor_off,
    logit,
    appearance,
    cam_linear,
    cam_shift,
    block_lists,
    pix_grad,
):
    columns = lax.axis_size("tiles")
    capacity = 4 * TPD * LIST // columns
    slot_count = columns * capacity
    channels = appearance.shape[0]
    geometry = jnp.concatenate([offsets, factor_diag, factor_off[None, :], logit[None, :]], axis=0)
    params = jnp.concatenate([geometry, appearance], axis=0)
    cams = lax.axis_size("cams")
    gathered = lax.all_to_all(
        jnp.broadcast_to(params[None], (cams,) + params.shape), "cams", 0, 0, tiled=True
    )
    params_col = gathered.transpose(1, 0, 2).reshape(params.shape[0], cams * params.shape[1])
    geometry_col = params_col[:6]
    appearance_col = params_col[6:]
    per_column = geometry_col.shape[1] // BLK
    linear = cam_linear[0]
    camera_shift = cam_shift[0]
    entries = block_lists.reshape(-1)
    entry_count = entries.shape[0]
    column, ranking, in_column = slot_ranks(entries, per_column, columns)
    entry_slot = column * capacity + ranking
    request = jnp.zeros((slot_count,), jnp.int32).at[entry_slot].set(in_column)
    wanted = lax.all_to_all(request, "tiles", split_axis=0, concat_axis=0, tiled=True)
    raw_params = geometry_col.reshape(6, per_column, BLK)[:, wanted].reshape(6, slot_count * BLK)
    raw_colours = appearance_col.reshape(channels, per_column, BLK)[:, wanted].reshape(
        channels, slot_count * BLK
    )
    send_proj = project(raw_params, linear, camera_shift).astype(jnp.bfloat16)
    sent = lax.all_to_all(
        jnp.concatenate([send_proj, raw_colours.astype(jnp.bfloat16)], axis=0),
        "tiles",
        split_axis=1,
        concat_axis=1,
        tiled=True,
    )
    rows = sent.shape[0]
    slot_hot = (jnp.arange(slot_count, dtype=jnp.int32)[:, None] == entry_slot[None, :]).astype(
        jnp.bfloat16
    )
    picked = jnp.einsum(
        "rsb,se->reb",
        sent.reshape(rows, slot_count, BLK),
        slot_hot,
        preferred_element_type=jnp.float32,
    ).reshape(rows, entry_count * BLK)
    projected = picked[:6]
    colours = picked[6:]
    cotangent = pix_grad.reshape(channels, TPD, -1).astype(jnp.float32)
    picture, grad_proj, grad_colour = tile_grads(projected, colours, cotangent)
    entry_grads = jnp.concatenate([grad_proj, grad_colour], axis=0).astype(jnp.bfloat16)
    back = jnp.einsum(
        "reb,se->rsb",
        entry_grads.reshape(rows, entry_count, BLK),
        slot_hot,
        preferred_element_type=jnp.float32,
    ).astype(jnp.bfloat16)
    returned = lax.all_to_all(
        back.reshape(rows, -1),
        "tiles",
        split_axis=1,
        concat_axis=1,
        tiled=True,
    )
    ret_proj = returned[:6]
    ret_colour = returned[6:]
    unused, pull_params = jax.vjp(lambda params: project(params, linear, camera_shift), raw_params)
    grad_raw = pull_params(ret_proj.astype(jnp.float32))[0]
    owner_hot = (wanted[:, None] == jnp.arange(per_column, dtype=jnp.int32)[None, :]).astype(
        jnp.float32
    )

    def collect(values, row_count):
        summed = jnp.einsum(
            "rsb,sk->rkb",
            values.reshape(row_count, slot_count, BLK),
            owner_hot,
            precision=lax.Precision.HIGHEST,
        )
        return summed.reshape(row_count, per_column * BLK)

    column_geometry = collect(grad_raw, 6)
    column_colour = collect(ret_colour.astype(jnp.float32), channels)
    column_all = jnp.concatenate([column_geometry, column_colour], axis=0)
    rows = column_all.shape[0]
    grads = lax.all_to_all(
        column_all.reshape(rows, cams, -1), "cams", 1, 1, tiled=True
    ).sum(axis=1)
    grad_geometry = grads[:6]
    grad_appearance = grads[6:]
    return (picture.reshape(channels, 1, -1), grad_geometry, grad_appearance)


def solution(mesh):
    return jax.shard_map(
        local,
        mesh=mesh,
        in_specs=(
            P(None, ("tiles", "cams")),
            P(None, ("tiles", "cams")),
            P(("tiles", "cams")),
            P(("tiles", "cams")),
            P(None, ("tiles", "cams")),
            P("cams", None),
            P("cams", None),
            P("cams", "tiles", None, None),
            P(None, "cams", "tiles"),
        ),
        out_specs=(
            P(None, "cams", "tiles"),
            P(None, ("tiles", "cams")),
            P(None, ("tiles", "cams")),
        ),
        check_vma=False,
    )
```

```python
import jax
import jax.numpy as jnp
from jax import lax
from jax.sharding import PartitionSpec as P

SIDE = 16
TPD = 16
LIST = 3
BLK = 8


def project(geometry, linear, camera_shift):
    lin_xx = 1.0 + linear[0]
    lin_xy = linear[1]
    lin_yx = linear[2]
    lin_yy = 1.0 + linear[3]
    diag_x = geometry[2]
    diag_y = geometry[3]
    lower = geometry[4]
    cov_xx = diag_x * diag_x
    cov_xy = diag_x * lower
    cov_yy = lower * lower + diag_y * diag_y
    half_xx = lin_xx * cov_xx + lin_xy * cov_xy
    half_xy = lin_xx * cov_xy + lin_xy * cov_yy
    half_yx = lin_yx * cov_xx + lin_yy * cov_xy
    half_yy = lin_yx * cov_xy + lin_yy * cov_yy
    img_xx = half_xx * lin_xx + half_xy * lin_xy + 0.3
    img_xy = half_xx * lin_yx + half_xy * lin_yy
    img_yy = half_yx * lin_yx + half_yy * lin_yy + 0.3
    determ = img_xx * img_yy - img_xy * img_xy
    centre_x = lin_xx * geometry[0] + lin_xy * geometry[1] + camera_shift[0]
    centre_y = lin_yx * geometry[0] + lin_yy * geometry[1] + camera_shift[1]
    opacity = 0.95 * jax.nn.sigmoid(geometry[5])
    return jnp.stack(
        [centre_x, centre_y, img_yy / determ, -img_xy / determ, img_xx / determ, opacity]
    )


def render_tile(projected, colours):
    pixels = jnp.arange(SIDE * SIDE)
    across = (pixels % SIDE).astype(jnp.float32) + 0.5 - SIDE / 2
    downward = (pixels // SIDE).astype(jnp.float32) + 0.5 - SIDE / 2
    delta_x = across[None, :] - projected[0][:, None]
    delta_y = downward[None, :] - projected[1][:, None]
    quadric = (
        projected[2][:, None] * delta_x * delta_x
        + 2.0 * projected[3][:, None] * delta_x * delta_y
        + projected[4][:, None] * delta_y * delta_y
    )
    coverage = projected[5][:, None] * jnp.exp(-0.5 * quadric)
    log_keep = jnp.log1p(-coverage)
    weight = jnp.exp(jnp.cumsum(log_keep, axis=0) - log_keep) * coverage
    return jnp.dot(
        colours, weight, precision=lax.Precision.HIGHEST, preferred_element_type=jnp.float32
    )


def tile_grads(projected, colours, cotangent):
    per_tile = projected.shape[1] // TPD
    channels = colours.shape[0]
    proj_tiles = projected.reshape(6, TPD, per_tile)
    colour_tiles = colours.reshape(channels, TPD, per_tile)

    def forward(proj_arg, colour_arg):
        return jax.vmap(render_tile, in_axes=(1, 1), out_axes=1)(proj_arg, colour_arg)

    picture, pullback = jax.vjp(forward, proj_tiles, colour_tiles)
    grad_proj, grad_colour = pullback(cotangent)
    return (picture, grad_proj.reshape(6, -1), grad_colour.reshape(channels, -1))


def slot_ranks(entries, blocks_per_column, columns):
    column = entries // blocks_per_column
    in_column = entries % blocks_per_column
    matches = (column[..., None] == jnp.arange(columns, dtype=jnp.int32)).astype(jnp.int32)
    before = jnp.cumsum(matches, axis=-2) - matches
    ranking = jnp.sum(before * matches, axis=-1)
    return (column, ranking, in_column)


def local(
    offsets,
    factor_diag,
    factor_off,
    logit,
    appearance,
    cam_linear,
    cam_shift,
    block_lists,
    pix_grad,
):
    columns = lax.axis_size("tiles")
    capacity = 4 * TPD * LIST // columns
    slot_count = columns * capacity
    channels = appearance.shape[0]
    geometry = jnp.concatenate([offsets, factor_diag, factor_off[None, :], logit[None, :]], axis=0)
    params = jnp.concatenate([geometry, appearance], axis=0)
    cams = lax.axis_size("cams")
    gathered = lax.all_to_all(
        jnp.broadcast_to(params[None], (cams,) + params.shape), "cams", 0, 0, tiled=True
    )
    params_col = gathered.transpose(1, 0, 2).reshape(params.shape[0], cams * params.shape[1])
    geometry_col = params_col[:6]
    appearance_col = params_col[6:]
    per_column = geometry_col.shape[1] // BLK
    linear = cam_linear[0]
    camera_shift = cam_shift[0]
    entries = block_lists.reshape(-1)
    entry_count = entries.shape[0]
    column, ranking, in_column = slot_ranks(entries, per_column, columns)
    entry_slot = column * capacity + ranking
    request = jnp.zeros((slot_count,), jnp.int32).at[entry_slot].set(in_column)
    wanted = lax.all_to_all(request, "tiles", split_axis=0, concat_axis=0, tiled=True)
    rows = params_col.shape[0]
    payload_col = jnp.concatenate(
        [project(geometry_col, linear, camera_shift), appearance_col], axis=0
    ).astype(jnp.bfloat16)
    owner_hot = (jnp.arange(per_column, dtype=jnp.int32)[:, None] == wanted[None, :]).astype(
        jnp.bfloat16
    )
    send = jnp.einsum(
        "rkb,ks->rbs",
        payload_col.reshape(rows, per_column, BLK),
        owner_hot,
        preferred_element_type=jnp.float32,
    ).astype(jnp.bfloat16)
    sent = lax.all_to_all(send, "tiles", split_axis=2, concat_axis=2, tiled=True)
    slot_hot = (jnp.arange(slot_count, dtype=jnp.int32)[:, None] == entry_slot[None, :]).astype(
        jnp.bfloat16
    )
    picked = jnp.einsum(
        "rbs,se->reb", sent, slot_hot, preferred_element_type=jnp.float32
    ).reshape(rows, entry_count * BLK)
    projected = picked[:6]
    colours = picked[6:]
    cotangent = pix_grad.reshape(channels, TPD, -1).astype(jnp.float32)
    picture, grad_proj, grad_colour = tile_grads(projected, colours, cotangent)
    entry_grads = jnp.concatenate([grad_proj, grad_colour], axis=0).astype(jnp.bfloat16)
    back = jnp.einsum(
        "reb,se->rbs",
        entry_grads.reshape(rows, entry_count, BLK),
        slot_hot,
        preferred_element_type=jnp.float32,
    ).astype(jnp.bfloat16)
    returned = lax.all_to_all(back, "tiles", split_axis=2, concat_axis=2, tiled=True)
    summed = jnp.einsum(
        "rbs,ks->rkb", returned, owner_hot, preferred_element_type=jnp.float32
    ).reshape(rows, per_column * BLK)
    unused, pull_params = jax.vjp(
        lambda params: project(params, linear, camera_shift), geometry_col
    )
    column_geometry = pull_params(summed[:6])[0]
    column_colour = summed[6:]
    column_all = jnp.concatenate([column_geometry, column_colour], axis=0)
    grads = lax.all_to_all(
        column_all.reshape(rows, cams, -1), "cams", 1, 1, tiled=True
    ).sum(axis=1)
    grad_geometry = grads[:6]
    grad_appearance = grads[6:]
    return (picture.reshape(channels, 1, -1), grad_geometry, grad_appearance)


def solution(mesh):
    return jax.shard_map(
        local,
        mesh=mesh,
        in_specs=(
            P(None, ("tiles", "cams")),
            P(None, ("tiles", "cams")),
            P(("tiles", "cams")),
            P(("tiles", "cams")),
            P(None, ("tiles", "cams")),
            P("cams", None),
            P("cams", None),
            P("cams", "tiles", None, None),
            P(None, "cams", "tiles"),
        ),
        out_specs=(
            P(None, "cams", "tiles"),
            P(None, ("tiles", "cams")),
            P(None, ("tiles", "cams")),
        ),
        check_vma=False,
    )
```

```python
import jax
import jax.numpy as jnp
from jax import lax
from jax.sharding import PartitionSpec as P

SIDE = 16
TPD = 16
LIST = 3
BLK = 8


def project(geometry, linear, camera_shift):
    lin_xx = 1.0 + linear[0]
    lin_xy = linear[1]
    lin_yx = linear[2]
    lin_yy = 1.0 + linear[3]
    diag_x = geometry[2]
    diag_y = geometry[3]
    lower = geometry[4]
    cov_xx = diag_x * diag_x
    cov_xy = diag_x * lower
    cov_yy = lower * lower + diag_y * diag_y
    half_xx = lin_xx * cov_xx + lin_xy * cov_xy
    half_xy = lin_xx * cov_xy + lin_xy * cov_yy
    half_yx = lin_yx * cov_xx + lin_yy * cov_xy
    half_yy = lin_yx * cov_xy + lin_yy * cov_yy
    img_xx = half_xx * lin_xx + half_xy * lin_xy + 0.3
    img_xy = half_xx * lin_yx + half_xy * lin_yy
    img_yy = half_yx * lin_yx + half_yy * lin_yy + 0.3
    determ = img_xx * img_yy - img_xy * img_xy
    centre_x = lin_xx * geometry[0] + lin_xy * geometry[1] + camera_shift[0]
    centre_y = lin_yx * geometry[0] + lin_yy * geometry[1] + camera_shift[1]
    opacity = 0.95 * jax.nn.sigmoid(geometry[5])
    return jnp.stack(
        [centre_x, centre_y, img_yy / determ, -img_xy / determ, img_xx / determ, opacity]
    )


def render_tile(projected, colours):
    pixels = jnp.arange(SIDE * SIDE)
    across = (pixels % SIDE).astype(jnp.float32) + 0.5 - SIDE / 2
    downward = (pixels // SIDE).astype(jnp.float32) + 0.5 - SIDE / 2
    delta_x = across[None, :] - projected[0][:, None]
    delta_y = downward[None, :] - projected[1][:, None]
    quadric = (
        projected[2][:, None] * delta_x * delta_x
        + 2.0 * projected[3][:, None] * delta_x * delta_y
        + projected[4][:, None] * delta_y * delta_y
    )
    coverage = projected[5][:, None] * jnp.exp(-0.5 * quadric)
    log_keep = jnp.log1p(-coverage)
    weight = jnp.exp(jnp.cumsum(log_keep, axis=0) - log_keep) * coverage
    return jnp.dot(
        colours, weight, precision=lax.Precision.HIGHEST, preferred_element_type=jnp.float32
    )


def tile_grads(projected, colours, cotangent):
    per_tile = projected.shape[1] // TPD
    channels = colours.shape[0]
    proj_tiles = projected.reshape(6, TPD, per_tile)
    colour_tiles = colours.reshape(channels, TPD, per_tile)

    def forward(proj_arg, colour_arg):
        return jax.vmap(render_tile, in_axes=(1, 1), out_axes=1)(proj_arg, colour_arg)

    picture, pullback = jax.vjp(forward, proj_tiles, colour_tiles)
    grad_proj, grad_colour = pullback(cotangent)
    return (picture, grad_proj.reshape(6, -1), grad_colour.reshape(channels, -1))


def slot_ranks(entries, blocks_per_column, columns):
    column = entries // blocks_per_column
    in_column = entries % blocks_per_column
    matches = (column[..., None] == jnp.arange(columns, dtype=jnp.int32)).astype(jnp.int32)
    before = jnp.cumsum(matches, axis=-2) - matches
    ranking = jnp.sum(before * matches, axis=-1)
    return (column, ranking, in_column)


def local(
    offsets,
    factor_diag,
    factor_off,
    logit,
    appearance,
    cam_linear,
    cam_shift,
    block_lists,
    pix_grad,
):
    columns = lax.axis_size("tiles")
    capacity = 4 * TPD * LIST // columns
    slot_count = columns * capacity
    channels = appearance.shape[0]
    geometry = jnp.concatenate([offsets, factor_diag, factor_off[None, :], logit[None, :]], axis=0)
    params = jnp.concatenate([geometry, appearance], axis=0)
    cams = lax.axis_size("cams")
    gathered = lax.all_to_all(
        jnp.broadcast_to(params[None], (cams,) + params.shape), "cams", 0, 0, tiled=True
    )
    params_col = gathered.transpose(1, 0, 2)
    geometry_col = params_col[:6]
    appearance_col = params_col[6:]
    per_column = cams * params.shape[1] // BLK
    local_blocks = params.shape[1] // BLK
    linear = cam_linear[0]
    camera_shift = cam_shift[0]
    entries = block_lists.reshape(-1)
    entry_count = entries.shape[0]
    column, ranking, in_column = slot_ranks(entries, per_column, columns)
    entry_slot = column * capacity + ranking
    request = jnp.zeros((slot_count,), jnp.int32).at[entry_slot].set(in_column)
    request, params_col = lax.optimization_barrier((request, params_col))
    wanted = lax.all_to_all(request, "tiles", split_axis=0, concat_axis=0, tiled=True)
    rows = params_col.shape[0]
    payload_col = jnp.concatenate(
        [project(geometry_col, linear, camera_shift), appearance_col], axis=0
    ).astype(jnp.bfloat16)
    owner_hot = (jnp.arange(per_column, dtype=jnp.int32)[:, None] == wanted[None, :]).astype(
        jnp.bfloat16
    )
    send = jnp.einsum(
        "rjlb,jls->rbs",
        payload_col.reshape(rows, cams, local_blocks, BLK),
        owner_hot.reshape(cams, local_blocks, slot_count),
        preferred_element_type=jnp.float32,
    ).astype(jnp.bfloat16)
    sent = lax.all_to_all(send, "tiles", split_axis=2, concat_axis=2, tiled=True)
    slot_hot = (jnp.arange(slot_count, dtype=jnp.int32)[:, None] == entry_slot[None, :]).astype(
        jnp.bfloat16
    )
    picked = jnp.einsum(
        "rbs,se->reb", sent, slot_hot, preferred_element_type=jnp.float32
    ).reshape(rows, entry_count * BLK)
    projected = picked[:6]
    colours = picked[6:]
    cotangent = pix_grad.reshape(channels, TPD, -1).astype(jnp.float32)
    picture, grad_proj, grad_colour = tile_grads(projected, colours, cotangent)
    entry_grads = jnp.concatenate([grad_proj, grad_colour], axis=0).astype(jnp.bfloat16)
    back = jnp.einsum(
        "reb,se->rbs",
        entry_grads.reshape(rows, entry_count, BLK),
        slot_hot,
        preferred_element_type=jnp.float32,
    ).astype(jnp.bfloat16)
    returned = lax.all_to_all(back, "tiles", split_axis=2, concat_axis=2, tiled=True)
    summed = jnp.einsum(
        "rbs,jls->rjlb",
        returned,
        owner_hot.reshape(cams, local_blocks, slot_count),
        preferred_element_type=jnp.float32,
    ).reshape(rows, cams, local_blocks * BLK)
    unused, pull_params = jax.vjp(
        lambda params: project(params, linear, camera_shift), geometry_col
    )
    column_geometry = pull_params(summed[:6])[0]
    column_colour = summed[6:]
    column_all = jnp.concatenate([column_geometry, column_colour], axis=0)
    grads = lax.all_to_all(column_all, "cams", 1, 1, tiled=True).sum(axis=1)
    grad_geometry = grads[:6]
    grad_appearance = grads[6:]
    return (picture.reshape(channels, 1, -1), grad_geometry, grad_appearance)


def solution(mesh):
    return jax.shard_map(
        local,
        mesh=mesh,
        in_specs=(
            P(None, ("tiles", "cams")),
            P(None, ("tiles", "cams")),
            P(("tiles", "cams")),
            P(("tiles", "cams")),
            P(None, ("tiles", "cams")),
            P("cams", None),
            P("cams", None),
            P("cams", "tiles", None, None),
            P(None, "cams", "tiles"),
        ),
        out_specs=(
            P(None, "cams", "tiles"),
            P(None, ("tiles", "cams")),
            P(None, ("tiles", "cams")),
        ),
        check_vma=False,
    )
```

```python
import jax
import jax.numpy as jnp
from jax import lax
from jax.sharding import PartitionSpec as P

SIDE = 16
TPD = 16
LIST = 3
BLK = 8


def project(geometry, linear, camera_shift):
    lin_xx = 1.0 + linear[0]
    lin_xy = linear[1]
    lin_yx = linear[2]
    lin_yy = 1.0 + linear[3]
    diag_x = geometry[2]
    diag_y = geometry[3]
    lower = geometry[4]
    cov_xx = diag_x * diag_x
    cov_xy = diag_x * lower
    cov_yy = lower * lower + diag_y * diag_y
    half_xx = lin_xx * cov_xx + lin_xy * cov_xy
    half_xy = lin_xx * cov_xy + lin_xy * cov_yy
    half_yx = lin_yx * cov_xx + lin_yy * cov_xy
    half_yy = lin_yx * cov_xy + lin_yy * cov_yy
    img_xx = half_xx * lin_xx + half_xy * lin_xy + 0.3
    img_xy = half_xx * lin_yx + half_xy * lin_yy
    img_yy = half_yx * lin_yx + half_yy * lin_yy + 0.3
    determ = img_xx * img_yy - img_xy * img_xy
    centre_x = lin_xx * geometry[0] + lin_xy * geometry[1] + camera_shift[0]
    centre_y = lin_yx * geometry[0] + lin_yy * geometry[1] + camera_shift[1]
    opacity = 0.95 * jax.nn.sigmoid(geometry[5])
    return jnp.stack(
        [centre_x, centre_y, img_yy / determ, -img_xy / determ, img_xx / determ, opacity]
    )


def project_pullback(geometry, linear, grad):
    lin_xx = 1.0 + linear[0]
    lin_xy = linear[1]
    lin_yx = linear[2]
    lin_yy = 1.0 + linear[3]
    diag_x = geometry[2]
    diag_y = geometry[3]
    lower = geometry[4]
    cov_xx = diag_x * diag_x
    cov_xy = diag_x * lower
    cov_yy = lower * lower + diag_y * diag_y
    half_xx = lin_xx * cov_xx + lin_xy * cov_xy
    half_xy = lin_xx * cov_xy + lin_xy * cov_yy
    half_yx = lin_yx * cov_xx + lin_yy * cov_xy
    half_yy = lin_yx * cov_xy + lin_yy * cov_yy
    img_xx = half_xx * lin_xx + half_xy * lin_xy + 0.3
    img_xy = half_xx * lin_yx + half_xy * lin_yy
    img_yy = half_yx * lin_yx + half_yy * lin_yy + 0.3
    determ = img_xx * img_yy - img_xy * img_xy
    inv = 1.0 / determ
    scale = (grad[2] * img_yy - grad[3] * img_xy + grad[4] * img_xx) * inv * inv
    g_xx = grad[4] * inv - scale * img_yy
    g_yy = grad[2] * inv - scale * img_xx
    g_xy = 2.0 * scale * img_xy - grad[3] * inv
    g_half_xx = g_xx * lin_xx + g_xy * lin_yx
    g_half_xy = g_xx * lin_xy + g_xy * lin_yy
    g_half_yx = g_yy * lin_yx
    g_half_yy = g_yy * lin_yy
    g_cov_xx = g_half_xx * lin_xx + g_half_yx * lin_yx
    g_cov_xy = g_half_xx * lin_xy + g_half_xy * lin_xx + g_half_yx * lin_yy + g_half_yy * lin_yx
    g_cov_yy = g_half_xy * lin_xy + g_half_yy * lin_yy
    opacity = jax.nn.sigmoid(geometry[5])
    return jnp.stack(
        [
            grad[0] * lin_xx + grad[1] * lin_yx,
            grad[0] * lin_xy + grad[1] * lin_yy,
            2.0 * g_cov_xx * diag_x + g_cov_xy * lower,
            2.0 * g_cov_yy * diag_y,
            g_cov_xy * diag_x + 2.0 * g_cov_yy * lower,
            grad[5] * 0.95 * opacity * (1.0 - opacity),
        ]
    )


def render_tile(projected, colours):
    pixels = jnp.arange(SIDE * SIDE)
    across = (pixels % SIDE).astype(jnp.float32) + 0.5 - SIDE / 2
    downward = (pixels // SIDE).astype(jnp.float32) + 0.5 - SIDE / 2
    delta_x = across[None, :] - projected[0][:, None]
    delta_y = downward[None, :] - projected[1][:, None]
    quadric = (
        projected[2][:, None] * delta_x * delta_x
        + 2.0 * projected[3][:, None] * delta_x * delta_y
        + projected[4][:, None] * delta_y * delta_y
    )
    coverage = projected[5][:, None] * jnp.exp(-0.5 * quadric)
    log_keep = jnp.log1p(-coverage)
    weight = jnp.exp(jnp.cumsum(log_keep, axis=0) - log_keep) * coverage
    return jnp.dot(
        colours, weight, precision=lax.Precision.HIGHEST, preferred_element_type=jnp.float32
    )


def tile_grads(projected, colours, cotangent):
    per_tile = projected.shape[1] // TPD
    channels = colours.shape[0]
    proj_tiles = projected.reshape(6, TPD, per_tile)
    colour_tiles = colours.reshape(channels, TPD, per_tile)

    def forward(proj_arg, colour_arg):
        return jax.vmap(render_tile, in_axes=(1, 1), out_axes=1)(proj_arg, colour_arg)

    picture, pullback = jax.vjp(forward, proj_tiles, colour_tiles)
    grad_proj, grad_colour = pullback(cotangent)
    return (picture, grad_proj.reshape(6, -1), grad_colour.reshape(channels, -1))


def slot_ranks(entries, blocks_per_column, columns):
    column = entries // blocks_per_column
    in_column = entries % blocks_per_column
    matches = (column[..., None] == jnp.arange(columns, dtype=jnp.int32)).astype(jnp.int32)
    before = jnp.cumsum(matches, axis=-2) - matches
    ranking = jnp.sum(before * matches, axis=-1)
    return (column, ranking, in_column)


def local(
    offsets,
    factor_diag,
    factor_off,
    logit,
    appearance,
    cam_linear,
    cam_shift,
    block_lists,
    pix_grad,
):
    columns = lax.axis_size("tiles")
    capacity = 4 * TPD * LIST // columns
    slot_count = columns * capacity
    channels = appearance.shape[0]
    geometry = jnp.concatenate([offsets, factor_diag, factor_off[None, :], logit[None, :]], axis=0)
    params = jnp.concatenate([geometry, appearance], axis=0)
    cams = lax.axis_size("cams")
    gathered = lax.all_to_all(
        jnp.broadcast_to(params[None], (cams,) + params.shape), "cams", 0, 0, tiled=True
    )
    params_col = gathered.transpose(1, 0, 2)
    geometry_col = params_col[:6]
    appearance_col = params_col[6:]
    per_column = cams * params.shape[1] // BLK
    local_blocks = params.shape[1] // BLK
    linear = cam_linear[0]
    camera_shift = cam_shift[0]
    entries = block_lists.reshape(-1)
    entry_count = entries.shape[0]
    column, ranking, in_column = slot_ranks(entries, per_column, columns)
    entry_slot = column * capacity + ranking
    request = jnp.zeros((slot_count,), jnp.int32).at[entry_slot].set(in_column)
    request, params_col = lax.optimization_barrier((request, params_col))
    wanted = lax.all_to_all(request, "tiles", split_axis=0, concat_axis=0, tiled=True)
    rows = params_col.shape[0]
    payload_col = jnp.concatenate(
        [project(geometry_col, linear, camera_shift), appearance_col], axis=0
    ).astype(jnp.bfloat16)
    owner_hot = (jnp.arange(per_column, dtype=jnp.int32)[:, None] == wanted[None, :]).astype(
        jnp.bfloat16
    )
    send = jnp.einsum(
        "rjlb,jls->rbs",
        payload_col.reshape(rows, cams, local_blocks, BLK),
        owner_hot.reshape(cams, local_blocks, slot_count),
        preferred_element_type=jnp.float32,
    ).astype(jnp.bfloat16)
    sent = lax.all_to_all(send, "tiles", split_axis=2, concat_axis=2, tiled=True)
    slot_hot = (jnp.arange(slot_count, dtype=jnp.int32)[:, None] == entry_slot[None, :]).astype(
        jnp.bfloat16
    )
    picked = jnp.einsum(
        "rbs,se->reb", sent, slot_hot, preferred_element_type=jnp.float32
    ).reshape(rows, entry_count * BLK)
    projected = picked[:6]
    colours = picked[6:]
    cotangent = pix_grad.reshape(channels, TPD, -1).astype(jnp.float32)
    picture, grad_proj, grad_colour = tile_grads(projected, colours, cotangent)
    entry_grads = jnp.concatenate([grad_proj, grad_colour], axis=0).astype(jnp.bfloat16)
    back = jnp.einsum(
        "reb,se->rbs",
        entry_grads.reshape(rows, entry_count, BLK),
        slot_hot,
        preferred_element_type=jnp.float32,
    ).astype(jnp.bfloat16)
    returned = lax.all_to_all(back, "tiles", split_axis=2, concat_axis=2, tiled=True)
    summed = jnp.einsum(
        "rbs,jls->rjlb",
        returned,
        owner_hot.reshape(cams, local_blocks, slot_count),
        preferred_element_type=jnp.float32,
    ).reshape(rows, cams, local_blocks * BLK)
    column_geometry = project_pullback(geometry_col, linear, summed[:6])
    column_colour = summed[6:]
    column_all = jnp.concatenate([column_geometry, column_colour], axis=0)
    grads = lax.all_to_all(column_all, "cams", 1, 1, tiled=True)
    grad_geometry = grads[:6].sum(axis=1)
    grad_appearance = grads[6:].sum(axis=1)
    return (picture.reshape(channels, 1, -1), grad_geometry, grad_appearance)


def solution(mesh):
    return jax.shard_map(
        local,
        mesh=mesh,
        in_specs=(
            P(None, ("tiles", "cams")),
            P(None, ("tiles", "cams")),
            P(("tiles", "cams")),
            P(("tiles", "cams")),
            P(None, ("tiles", "cams")),
            P("cams", None),
            P("cams", None),
            P("cams", "tiles", None, None),
            P(None, "cams", "tiles"),
        ),
        out_specs=(
            P(None, "cams", "tiles"),
            P(None, ("tiles", "cams")),
            P(None, ("tiles", "cams")),
        ),
        check_vma=False,
    )
```

```python
import jax
import jax.numpy as jnp
from jax import lax
from jax.sharding import PartitionSpec as P

SIDE = 16
TPD = 16
LIST = 3
BLK = 8


def project(geometry, linear, camera_shift):
    lin_xx = 1.0 + linear[0]
    lin_xy = linear[1]
    lin_yx = linear[2]
    lin_yy = 1.0 + linear[3]
    diag_x = geometry[2]
    diag_y = geometry[3]
    lower = geometry[4]
    cov_xx = diag_x * diag_x
    cov_xy = diag_x * lower
    cov_yy = lower * lower + diag_y * diag_y
    half_xx = lin_xx * cov_xx + lin_xy * cov_xy
    half_xy = lin_xx * cov_xy + lin_xy * cov_yy
    half_yx = lin_yx * cov_xx + lin_yy * cov_xy
    half_yy = lin_yx * cov_xy + lin_yy * cov_yy
    img_xx = half_xx * lin_xx + half_xy * lin_xy + 0.3
    img_xy = half_xx * lin_yx + half_xy * lin_yy
    img_yy = half_yx * lin_yx + half_yy * lin_yy + 0.3
    determ = img_xx * img_yy - img_xy * img_xy
    centre_x = lin_xx * geometry[0] + lin_xy * geometry[1] + camera_shift[0]
    centre_y = lin_yx * geometry[0] + lin_yy * geometry[1] + camera_shift[1]
    opacity = 0.95 * jax.nn.sigmoid(geometry[5])
    return jnp.stack(
        [centre_x, centre_y, img_yy / determ, -img_xy / determ, img_xx / determ, opacity]
    )


def project_pullback(geometry, linear, grad):
    lin_xx = 1.0 + linear[0]
    lin_xy = linear[1]
    lin_yx = linear[2]
    lin_yy = 1.0 + linear[3]
    diag_x = geometry[2]
    diag_y = geometry[3]
    lower = geometry[4]
    cov_xx = diag_x * diag_x
    cov_xy = diag_x * lower
    cov_yy = lower * lower + diag_y * diag_y
    half_xx = lin_xx * cov_xx + lin_xy * cov_xy
    half_xy = lin_xx * cov_xy + lin_xy * cov_yy
    half_yx = lin_yx * cov_xx + lin_yy * cov_xy
    half_yy = lin_yx * cov_xy + lin_yy * cov_yy
    img_xx = half_xx * lin_xx + half_xy * lin_xy + 0.3
    img_xy = half_xx * lin_yx + half_xy * lin_yy
    img_yy = half_yx * lin_yx + half_yy * lin_yy + 0.3
    determ = img_xx * img_yy - img_xy * img_xy
    inv = 1.0 / determ
    scale = (grad[2] * img_yy - grad[3] * img_xy + grad[4] * img_xx) * inv * inv
    g_xx = grad[4] * inv - scale * img_yy
    g_yy = grad[2] * inv - scale * img_xx
    g_xy = 2.0 * scale * img_xy - grad[3] * inv
    g_half_xx = g_xx * lin_xx + g_xy * lin_yx
    g_half_xy = g_xx * lin_xy + g_xy * lin_yy
    g_half_yx = g_yy * lin_yx
    g_half_yy = g_yy * lin_yy
    g_cov_xx = g_half_xx * lin_xx + g_half_yx * lin_yx
    g_cov_xy = g_half_xx * lin_xy + g_half_xy * lin_xx + g_half_yx * lin_yy + g_half_yy * lin_yx
    g_cov_yy = g_half_xy * lin_xy + g_half_yy * lin_yy
    opacity = jax.nn.sigmoid(geometry[5])
    return jnp.stack(
        [
            grad[0] * lin_xx + grad[1] * lin_yx,
            grad[0] * lin_xy + grad[1] * lin_yy,
            2.0 * g_cov_xx * diag_x + g_cov_xy * lower,
            2.0 * g_cov_yy * diag_y,
            g_cov_xy * diag_x + 2.0 * g_cov_yy * lower,
            grad[5] * 0.95 * opacity * (1.0 - opacity),
        ]
    )


def render_tile(projected, colours):
    pixels = jnp.arange(SIDE * SIDE)
    across = (pixels % SIDE).astype(jnp.float32) + 0.5 - SIDE / 2
    downward = (pixels // SIDE).astype(jnp.float32) + 0.5 - SIDE / 2
    delta_x = across[None, :] - projected[0][:, None]
    delta_y = downward[None, :] - projected[1][:, None]
    quadric = (
        projected[2][:, None] * delta_x * delta_x
        + 2.0 * projected[3][:, None] * delta_x * delta_y
        + projected[4][:, None] * delta_y * delta_y
    )
    coverage = projected[5][:, None] * jnp.exp(-0.5 * quadric)
    log_keep = jnp.log1p(-coverage)
    weight = jnp.exp(jnp.cumsum(log_keep, axis=0) - log_keep) * coverage
    return jnp.dot(
        colours, weight, precision=lax.Precision.HIGHEST, preferred_element_type=jnp.float32
    )


def tile_grads(projected, colours, cotangent):
    per_tile = projected.shape[1] // TPD
    channels = colours.shape[0]
    proj_tiles = projected.reshape(6, TPD, per_tile)
    colour_tiles = colours.reshape(channels, TPD, per_tile)

    def forward(proj_arg, colour_arg):
        return jax.vmap(render_tile, in_axes=(1, 1), out_axes=1)(proj_arg, colour_arg)

    picture, pullback = jax.vjp(forward, proj_tiles, colour_tiles)
    grad_proj, grad_colour = pullback(cotangent)
    return (picture, grad_proj.reshape(6, -1), grad_colour.reshape(channels, -1))


def slot_ranks(entries, blocks_per_column, columns):
    column = entries // blocks_per_column
    in_column = entries % blocks_per_column
    matches = (column[..., None] == jnp.arange(columns, dtype=jnp.int32)).astype(jnp.int32)
    before = jnp.cumsum(matches, axis=-2) - matches
    ranking = jnp.sum(before * matches, axis=-1)
    return (column, ranking, in_column)


def local(
    offsets,
    factor_diag,
    factor_off,
    logit,
    appearance,
    cam_linear,
    cam_shift,
    block_lists,
    pix_grad,
):
    columns = lax.axis_size("tiles")
    capacity = 4 * TPD * LIST // columns
    slot_count = columns * capacity
    channels = appearance.shape[0]
    geometry = jnp.concatenate([offsets, factor_diag, factor_off[None, :], logit[None, :]], axis=0)
    params = jnp.concatenate([geometry, appearance], axis=0)
    cams = lax.axis_size("cams")
    local_blocks = params.shape[1] // BLK
    per_column = cams * local_blocks
    by_lane = params.reshape(params.shape[0], local_blocks, BLK).transpose(0, 2, 1)
    gathered = lax.all_to_all(
        jnp.broadcast_to(by_lane[None], (cams,) + by_lane.shape), "cams", 0, 0, tiled=True
    )
    params_col = gathered.transpose(1, 2, 0, 3).reshape(params.shape[0], BLK, per_column)
    geometry_col = params_col[:6]
    appearance_col = params_col[6:]
    linear = cam_linear[0]
    camera_shift = cam_shift[0]
    entries = block_lists.reshape(-1)
    entry_count = entries.shape[0]
    column, ranking, in_column = slot_ranks(entries, per_column, columns)
    entry_slot = column * capacity + ranking
    request = jnp.zeros((slot_count,), jnp.int32).at[entry_slot].set(in_column)
    request, params_col = lax.optimization_barrier((request, params_col))
    wanted = lax.all_to_all(request, "tiles", split_axis=0, concat_axis=0, tiled=True)
    rows = params_col.shape[0]
    payload_col = jnp.concatenate(
        [project(geometry_col, linear, camera_shift), appearance_col], axis=0
    ).astype(jnp.bfloat16)
    owner_hot = (jnp.arange(per_column, dtype=jnp.int32)[:, None] == wanted[None, :]).astype(
        jnp.bfloat16
    )
    send = jnp.einsum(
        "rbk,ks->rbs",
        payload_col,
        owner_hot,
        preferred_element_type=jnp.float32,
    ).astype(jnp.bfloat16)
    sent = lax.all_to_all(send, "tiles", split_axis=2, concat_axis=2, tiled=True)
    slot_hot = (jnp.arange(slot_count, dtype=jnp.int32)[:, None] == entry_slot[None, :]).astype(
        jnp.bfloat16
    )
    picked = jnp.einsum(
        "rbs,se->reb", sent, slot_hot, preferred_element_type=jnp.float32
    ).reshape(rows, entry_count * BLK)
    projected = picked[:6]
    colours = picked[6:]
    cotangent = pix_grad.reshape(channels, TPD, -1).astype(jnp.float32)
    picture, grad_proj, grad_colour = tile_grads(projected, colours, cotangent)
    entry_grads = jnp.concatenate([grad_proj, grad_colour], axis=0).astype(jnp.bfloat16)
    back = jnp.einsum(
        "reb,se->rbs",
        entry_grads.reshape(rows, entry_count, BLK),
        slot_hot,
        preferred_element_type=jnp.float32,
    ).astype(jnp.bfloat16)
    returned = lax.all_to_all(back, "tiles", split_axis=2, concat_axis=2, tiled=True)
    summed = jnp.einsum("rbs,ks->rbk", returned, owner_hot, preferred_element_type=jnp.float32)
    column_geometry = project_pullback(geometry_col, linear, summed[:6])
    column_colour = summed[6:]
    column_all = jnp.concatenate([column_geometry, column_colour], axis=0)
    grads = lax.all_to_all(
        column_all.reshape(rows, BLK, cams, local_blocks), "cams", 2, 2, tiled=True
    ).sum(axis=2)
    grads = grads.transpose(0, 2, 1).reshape(rows, local_blocks * BLK)
    grad_geometry = grads[:6]
    grad_appearance = grads[6:]
    return (picture.reshape(channels, 1, -1), grad_geometry, grad_appearance)


def solution(mesh):
    return jax.shard_map(
        local,
        mesh=mesh,
        in_specs=(
            P(None, ("tiles", "cams")),
            P(None, ("tiles", "cams")),
            P(("tiles", "cams")),
            P(("tiles", "cams")),
            P(None, ("tiles", "cams")),
            P("cams", None),
            P("cams", None),
            P("cams", "tiles", None, None),
            P(None, "cams", "tiles"),
        ),
        out_specs=(
            P(None, "cams", "tiles"),
            P(None, ("tiles", "cams")),
            P(None, ("tiles", "cams")),
        ),
        check_vma=False,
    )
```

```python
import jax
import jax.numpy as jnp
from jax import lax
from jax.sharding import PartitionSpec as P

SIDE = 16
TPD = 16
LIST = 3
BLK = 8


def project(geometry, linear, camera_shift):
    lin_xx = 1.0 + linear[0]
    lin_xy = linear[1]
    lin_yx = linear[2]
    lin_yy = 1.0 + linear[3]
    diag_x = geometry[2]
    diag_y = geometry[3]
    lower = geometry[4]
    cov_xx = diag_x * diag_x
    cov_xy = diag_x * lower
    cov_yy = lower * lower + diag_y * diag_y
    half_xx = lin_xx * cov_xx + lin_xy * cov_xy
    half_xy = lin_xx * cov_xy + lin_xy * cov_yy
    half_yx = lin_yx * cov_xx + lin_yy * cov_xy
    half_yy = lin_yx * cov_xy + lin_yy * cov_yy
    img_xx = half_xx * lin_xx + half_xy * lin_xy + 0.3
    img_xy = half_xx * lin_yx + half_xy * lin_yy
    img_yy = half_yx * lin_yx + half_yy * lin_yy + 0.3
    determ = img_xx * img_yy - img_xy * img_xy
    centre_x = lin_xx * geometry[0] + lin_xy * geometry[1] + camera_shift[0]
    centre_y = lin_yx * geometry[0] + lin_yy * geometry[1] + camera_shift[1]
    opacity = 0.95 * jax.nn.sigmoid(geometry[5])
    return jnp.stack(
        [centre_x, centre_y, img_yy / determ, -img_xy / determ, img_xx / determ, opacity]
    )


def project_pullback(geometry, linear, grad):
    lin_xx = 1.0 + linear[0]
    lin_xy = linear[1]
    lin_yx = linear[2]
    lin_yy = 1.0 + linear[3]
    diag_x = geometry[2]
    diag_y = geometry[3]
    lower = geometry[4]
    cov_xx = diag_x * diag_x
    cov_xy = diag_x * lower
    cov_yy = lower * lower + diag_y * diag_y
    half_xx = lin_xx * cov_xx + lin_xy * cov_xy
    half_xy = lin_xx * cov_xy + lin_xy * cov_yy
    half_yx = lin_yx * cov_xx + lin_yy * cov_xy
    half_yy = lin_yx * cov_xy + lin_yy * cov_yy
    img_xx = half_xx * lin_xx + half_xy * lin_xy + 0.3
    img_xy = half_xx * lin_yx + half_xy * lin_yy
    img_yy = half_yx * lin_yx + half_yy * lin_yy + 0.3
    determ = img_xx * img_yy - img_xy * img_xy
    inv = 1.0 / determ
    scale = (grad[2] * img_yy - grad[3] * img_xy + grad[4] * img_xx) * inv * inv
    g_xx = grad[4] * inv - scale * img_yy
    g_yy = grad[2] * inv - scale * img_xx
    g_xy = 2.0 * scale * img_xy - grad[3] * inv
    g_half_xx = g_xx * lin_xx + g_xy * lin_yx
    g_half_xy = g_xx * lin_xy + g_xy * lin_yy
    g_half_yx = g_yy * lin_yx
    g_half_yy = g_yy * lin_yy
    g_cov_xx = g_half_xx * lin_xx + g_half_yx * lin_yx
    g_cov_xy = g_half_xx * lin_xy + g_half_xy * lin_xx + g_half_yx * lin_yy + g_half_yy * lin_yx
    g_cov_yy = g_half_xy * lin_xy + g_half_yy * lin_yy
    opacity = jax.nn.sigmoid(geometry[5])
    return jnp.stack(
        [
            grad[0] * lin_xx + grad[1] * lin_yx,
            grad[0] * lin_xy + grad[1] * lin_yy,
            2.0 * g_cov_xx * diag_x + g_cov_xy * lower,
            2.0 * g_cov_yy * diag_y,
            g_cov_xy * diag_x + 2.0 * g_cov_yy * lower,
            grad[5] * 0.95 * opacity * (1.0 - opacity),
        ]
    )


def render_tile(projected, colours):
    pixels = jnp.arange(SIDE * SIDE)
    across = (pixels % SIDE).astype(jnp.float32) + 0.5 - SIDE / 2
    downward = (pixels // SIDE).astype(jnp.float32) + 0.5 - SIDE / 2
    delta_x = across[None, :] - projected[0][:, None]
    delta_y = downward[None, :] - projected[1][:, None]
    quadric = (
        projected[2][:, None] * delta_x * delta_x
        + 2.0 * projected[3][:, None] * delta_x * delta_y
        + projected[4][:, None] * delta_y * delta_y
    )
    coverage = projected[5][:, None] * jnp.exp(-0.5 * quadric)
    log_keep = jnp.log1p(-coverage)
    weight = jnp.exp(jnp.cumsum(log_keep, axis=0) - log_keep) * coverage
    return jnp.dot(
        colours, weight, precision=lax.Precision.HIGHEST, preferred_element_type=jnp.float32
    )


def tile_grads(projected, colours, cotangent):
    per_tile = projected.shape[1] // TPD
    channels = colours.shape[0]
    proj_tiles = projected.reshape(6, TPD, per_tile)
    colour_tiles = colours.reshape(channels, TPD, per_tile)

    def forward(proj_arg, colour_arg):
        return jax.vmap(render_tile, in_axes=(1, 1), out_axes=1)(proj_arg, colour_arg)

    picture, pullback = jax.vjp(forward, proj_tiles, colour_tiles)
    grad_proj, grad_colour = pullback(cotangent)
    return (picture, grad_proj.reshape(6, -1), grad_colour.reshape(channels, -1))


def slot_ranks(entries, blocks_per_column, columns):
    column = entries // blocks_per_column
    in_column = entries % blocks_per_column
    matches = (column[..., None] == jnp.arange(columns, dtype=jnp.int32)).astype(jnp.int32)
    before = jnp.cumsum(matches, axis=-2) - matches
    ranking = jnp.sum(before * matches, axis=-1)
    return (column, ranking, in_column)


def local(
    offsets,
    factor_diag,
    factor_off,
    logit,
    appearance,
    cam_linear,
    cam_shift,
    block_lists,
    pix_grad,
):
    columns = lax.axis_size("tiles")
    capacity = 4 * TPD * LIST // columns
    slot_count = columns * capacity
    channels = appearance.shape[0]
    geometry = jnp.concatenate([offsets, factor_diag, factor_off[None, :], logit[None, :]], axis=0)
    params = jnp.concatenate([geometry, appearance], axis=0)
    cams = lax.axis_size("cams")
    local_blocks = params.shape[1] // BLK
    per_column = cams * local_blocks
    by_lane = params.reshape(params.shape[0], local_blocks, BLK).transpose(0, 2, 1)
    gathered = lax.all_to_all(
        jnp.broadcast_to(by_lane[None], (cams,) + by_lane.shape), "cams", 0, 0, tiled=True
    )
    params_col = gathered.transpose(1, 2, 0, 3).reshape(params.shape[0], BLK, per_column)
    linear = cam_linear[0]
    camera_shift = cam_shift[0]
    entries = block_lists.reshape(-1)
    entry_count = entries.shape[0]
    column, ranking, in_column = slot_ranks(entries, per_column, columns)
    entry_slot = column * capacity + ranking
    request = jnp.zeros((slot_count,), jnp.int32).at[entry_slot].set(in_column)
    request, params_col = lax.optimization_barrier((request, params_col))
    geometry_col = params_col[:6]
    appearance_col = params_col[6:]
    wanted = lax.all_to_all(request, "tiles", split_axis=0, concat_axis=0, tiled=True)
    rows = params_col.shape[0]
    payload_col = jnp.concatenate(
        [project(geometry_col, linear, camera_shift), appearance_col], axis=0
    ).astype(jnp.bfloat16)
    owner_hot = (jnp.arange(per_column, dtype=jnp.int32)[:, None] == wanted[None, :]).astype(
        jnp.bfloat16
    )
    send = jnp.einsum(
        "rbk,ks->rbs",
        payload_col,
        owner_hot,
        preferred_element_type=jnp.float32,
    ).astype(jnp.bfloat16)
    sent = lax.all_to_all(send, "tiles", split_axis=2, concat_axis=2, tiled=True)
    slot_hot = (jnp.arange(slot_count, dtype=jnp.int32)[:, None] == entry_slot[None, :]).astype(
        jnp.bfloat16
    )
    picked = jnp.einsum(
        "rbs,se->reb", sent, slot_hot, preferred_element_type=jnp.float32
    ).reshape(rows, entry_count * BLK)
    projected = picked[:6]
    colours = picked[6:]
    cotangent = pix_grad.reshape(channels, TPD, -1).astype(jnp.float32)
    picture, grad_proj, grad_colour = tile_grads(projected, colours, cotangent)
    entry_grads = jnp.concatenate([grad_proj, grad_colour], axis=0).astype(jnp.bfloat16)
    back = jnp.einsum(
        "reb,se->rbs",
        entry_grads.reshape(rows, entry_count, BLK),
        slot_hot,
        preferred_element_type=jnp.float32,
    ).astype(jnp.bfloat16)
    returned = lax.all_to_all(back, "tiles", split_axis=2, concat_axis=2, tiled=True)
    summed = jnp.einsum("rbs,ks->rbk", returned, owner_hot, preferred_element_type=jnp.float32)
    column_geometry = project_pullback(geometry_col, linear, summed[:6])
    column_colour = summed[6:]
    column_all = jnp.concatenate([column_geometry, column_colour], axis=0)
    grads = lax.all_to_all(
        column_all.reshape(rows, BLK, cams, local_blocks), "cams", 2, 2, tiled=True
    ).sum(axis=2)
    grads = grads.transpose(0, 2, 1).reshape(rows, local_blocks * BLK)
    grad_geometry = grads[:6]
    grad_appearance = grads[6:]
    return (picture.reshape(channels, 1, -1), grad_geometry, grad_appearance)


def solution(mesh):
    return jax.shard_map(
        local,
        mesh=mesh,
        in_specs=(
            P(None, ("tiles", "cams")),
            P(None, ("tiles", "cams")),
            P(("tiles", "cams")),
            P(("tiles", "cams")),
            P(None, ("tiles", "cams")),
            P("cams", None),
            P("cams", None),
            P("cams", "tiles", None, None),
            P(None, "cams", "tiles"),
        ),
        out_specs=(
            P(None, "cams", "tiles"),
            P(None, ("tiles", "cams")),
            P(None, ("tiles", "cams")),
        ),
        check_vma=False,
    )
```

```python
import jax
import jax.numpy as jnp
from jax import lax
from jax.sharding import PartitionSpec as P

SIDE = 16
TPD = 16
LIST = 3
BLK = 8


def project(geometry, linear, camera_shift):
    lin_xx = 1.0 + linear[0]
    lin_xy = linear[1]
    lin_yx = linear[2]
    lin_yy = 1.0 + linear[3]
    diag_x = geometry[2]
    diag_y = geometry[3]
    lower = geometry[4]
    cov_xx = diag_x * diag_x
    cov_xy = diag_x * lower
    cov_yy = lower * lower + diag_y * diag_y
    half_xx = lin_xx * cov_xx + lin_xy * cov_xy
    half_xy = lin_xx * cov_xy + lin_xy * cov_yy
    half_yx = lin_yx * cov_xx + lin_yy * cov_xy
    half_yy = lin_yx * cov_xy + lin_yy * cov_yy
    img_xx = half_xx * lin_xx + half_xy * lin_xy + 0.3
    img_xy = half_xx * lin_yx + half_xy * lin_yy
    img_yy = half_yx * lin_yx + half_yy * lin_yy + 0.3
    determ = img_xx * img_yy - img_xy * img_xy
    centre_x = lin_xx * geometry[0] + lin_xy * geometry[1] + camera_shift[0]
    centre_y = lin_yx * geometry[0] + lin_yy * geometry[1] + camera_shift[1]
    opacity = 0.95 * jax.nn.sigmoid(geometry[5])
    return jnp.stack(
        [centre_x, centre_y, img_yy / determ, -img_xy / determ, img_xx / determ, opacity]
    )


def project_pullback(geometry, linear, grad):
    lin_xx = 1.0 + linear[0]
    lin_xy = linear[1]
    lin_yx = linear[2]
    lin_yy = 1.0 + linear[3]
    diag_x = geometry[2]
    diag_y = geometry[3]
    lower = geometry[4]
    cov_xx = diag_x * diag_x
    cov_xy = diag_x * lower
    cov_yy = lower * lower + diag_y * diag_y
    half_xx = lin_xx * cov_xx + lin_xy * cov_xy
    half_xy = lin_xx * cov_xy + lin_xy * cov_yy
    half_yx = lin_yx * cov_xx + lin_yy * cov_xy
    half_yy = lin_yx * cov_xy + lin_yy * cov_yy
    img_xx = half_xx * lin_xx + half_xy * lin_xy + 0.3
    img_xy = half_xx * lin_yx + half_xy * lin_yy
    img_yy = half_yx * lin_yx + half_yy * lin_yy + 0.3
    determ = img_xx * img_yy - img_xy * img_xy
    inv = 1.0 / determ
    scale = (grad[2] * img_yy - grad[3] * img_xy + grad[4] * img_xx) * inv * inv
    g_xx = grad[4] * inv - scale * img_yy
    g_yy = grad[2] * inv - scale * img_xx
    g_xy = 2.0 * scale * img_xy - grad[3] * inv
    g_half_xx = g_xx * lin_xx + g_xy * lin_yx
    g_half_xy = g_xx * lin_xy + g_xy * lin_yy
    g_half_yx = g_yy * lin_yx
    g_half_yy = g_yy * lin_yy
    g_cov_xx = g_half_xx * lin_xx + g_half_yx * lin_yx
    g_cov_xy = g_half_xx * lin_xy + g_half_xy * lin_xx + g_half_yx * lin_yy + g_half_yy * lin_yx
    g_cov_yy = g_half_xy * lin_xy + g_half_yy * lin_yy
    opacity = jax.nn.sigmoid(geometry[5])
    return jnp.stack(
        [
            grad[0] * lin_xx + grad[1] * lin_yx,
            grad[0] * lin_xy + grad[1] * lin_yy,
            2.0 * g_cov_xx * diag_x + g_cov_xy * lower,
            2.0 * g_cov_yy * diag_y,
            g_cov_xy * diag_x + 2.0 * g_cov_yy * lower,
            grad[5] * 0.95 * opacity * (1.0 - opacity),
        ]
    )


def render_tile(projected, colours):
    pixels = jnp.arange(SIDE * SIDE)
    across = (pixels % SIDE).astype(jnp.float32) + 0.5 - SIDE / 2
    downward = (pixels // SIDE).astype(jnp.float32) + 0.5 - SIDE / 2
    delta_x = across[None, :] - projected[0][:, None]
    delta_y = downward[None, :] - projected[1][:, None]
    quadric = (
        projected[2][:, None] * delta_x * delta_x
        + 2.0 * projected[3][:, None] * delta_x * delta_y
        + projected[4][:, None] * delta_y * delta_y
    )
    coverage = projected[5][:, None] * jnp.exp(-0.5 * quadric)
    log_keep = jnp.log1p(-coverage)
    weight = jnp.exp(jnp.cumsum(log_keep, axis=0) - log_keep) * coverage
    return jnp.dot(
        colours, weight, precision=lax.Precision.HIGHEST, preferred_element_type=jnp.float32
    )


def tile_grads(projected, colours, cotangent):
    per_tile = projected.shape[1] // TPD
    channels = colours.shape[0]
    proj_tiles = projected.reshape(6, TPD, per_tile)
    colour_tiles = colours.reshape(channels, TPD, per_tile)

    def forward(proj_arg, colour_arg):
        return jax.vmap(render_tile, in_axes=(1, 1), out_axes=1)(proj_arg, colour_arg)

    picture, pullback = jax.vjp(forward, proj_tiles, colour_tiles)
    grad_proj, grad_colour = pullback(cotangent)
    return (picture, grad_proj.reshape(6, -1), grad_colour.reshape(channels, -1))


def tile_grads_direct(projected, colours, cotangent):
    channels = colours.shape[0]
    proj = projected.reshape(6, TPD, -1)
    colour_tiles = colours.reshape(channels, TPD, -1)
    pixels = jnp.arange(SIDE * SIDE)
    across = (pixels % SIDE).astype(jnp.float32) + 0.5 - SIDE / 2
    downward = (pixels // SIDE).astype(jnp.float32) + 0.5 - SIDE / 2
    delta_x = across[None, None, :] - proj[0][..., None]
    delta_y = downward[None, None, :] - proj[1][..., None]
    conic_0 = proj[2][..., None]
    conic_1 = proj[3][..., None]
    conic_2 = proj[4][..., None]
    quadric = (
        conic_0 * delta_x * delta_x
        + 2.0 * conic_1 * delta_x * delta_y
        + conic_2 * delta_y * delta_y
    )
    falloff = jnp.exp(-0.5 * quadric)
    coverage = proj[5][..., None] * falloff
    log_keep = jnp.log1p(-coverage)
    keep = jnp.exp(jnp.cumsum(log_keep, axis=1) - log_keep)
    weight = keep * coverage
    hi = lax.Precision.HIGHEST
    picture = jnp.einsum("cti,tip->ctp", colour_tiles, weight, precision=hi)
    grad_colour = jnp.einsum("ctp,tip->cti", cotangent, weight, precision=hi)
    grad_weight = jnp.einsum("cti,ctp->tip", colour_tiles, cotangent, precision=hi)
    grad_sum = grad_weight * weight
    grad_log = jnp.sum(grad_sum, axis=1, keepdims=True) - jnp.cumsum(grad_sum, axis=1)
    grad_cover = grad_weight * keep - grad_log / (1.0 - coverage)
    grad_quad = -0.5 * grad_cover * coverage
    grad_proj = jnp.stack(
        [
            -jnp.sum(grad_quad * (2.0 * conic_0 * delta_x + 2.0 * conic_1 * delta_y), axis=2),
            -jnp.sum(grad_quad * (2.0 * conic_1 * delta_x + 2.0 * conic_2 * delta_y), axis=2),
            jnp.sum(grad_quad * delta_x * delta_x, axis=2),
            jnp.sum(2.0 * grad_quad * delta_x * delta_y, axis=2),
            jnp.sum(grad_quad * delta_y * delta_y, axis=2),
            jnp.sum(grad_cover * falloff, axis=2),
        ]
    )
    return (picture, grad_proj.reshape(6, -1), grad_colour.reshape(channels, -1))


def slot_ranks(entries, blocks_per_column, columns):
    column = entries // blocks_per_column
    in_column = entries % blocks_per_column
    matches = (column[..., None] == jnp.arange(columns, dtype=jnp.int32)).astype(jnp.int32)
    before = jnp.cumsum(matches, axis=-2) - matches
    ranking = jnp.sum(before * matches, axis=-1)
    return (column, ranking, in_column)


def local(
    offsets,
    factor_diag,
    factor_off,
    logit,
    appearance,
    cam_linear,
    cam_shift,
    block_lists,
    pix_grad,
):
    columns = lax.axis_size("tiles")
    capacity = 4 * TPD * LIST // columns
    slot_count = columns * capacity
    channels = appearance.shape[0]
    geometry = jnp.concatenate([offsets, factor_diag, factor_off[None, :], logit[None, :]], axis=0)
    params = jnp.concatenate([geometry, appearance], axis=0)
    cams = lax.axis_size("cams")
    local_blocks = params.shape[1] // BLK
    per_column = cams * local_blocks
    by_lane = params.reshape(params.shape[0], local_blocks, BLK).transpose(0, 2, 1)
    gathered = lax.all_to_all(
        jnp.broadcast_to(by_lane[None], (cams,) + by_lane.shape), "cams", 0, 0, tiled=True
    )
    params_col = gathered.transpose(1, 2, 0, 3).reshape(params.shape[0], BLK, per_column)
    linear = cam_linear[0]
    camera_shift = cam_shift[0]
    entries = block_lists.reshape(-1)
    entry_count = entries.shape[0]
    column, ranking, in_column = slot_ranks(entries, per_column, columns)
    entry_slot = column * capacity + ranking
    request = jnp.zeros((slot_count,), jnp.int32).at[entry_slot].set(in_column)
    request, params_col = lax.optimization_barrier((request, params_col))
    geometry_col = params_col[:6]
    appearance_col = params_col[6:]
    wanted = lax.all_to_all(request, "tiles", split_axis=0, concat_axis=0, tiled=True)
    rows = params_col.shape[0]
    payload_col = jnp.concatenate(
        [project(geometry_col, linear, camera_shift), appearance_col], axis=0
    ).astype(jnp.bfloat16)
    owner_hot = (jnp.arange(per_column, dtype=jnp.int32)[:, None] == wanted[None, :]).astype(
        jnp.bfloat16
    )
    send = jnp.einsum(
        "rbk,ks->rbs",
        payload_col,
        owner_hot,
        preferred_element_type=jnp.float32,
    ).astype(jnp.bfloat16)
    sent = lax.all_to_all(send, "tiles", split_axis=2, concat_axis=2, tiled=True)
    slot_hot = (jnp.arange(slot_count, dtype=jnp.int32)[:, None] == entry_slot[None, :]).astype(
        jnp.bfloat16
    )
    picked = jnp.einsum(
        "rbs,se->reb", sent, slot_hot, preferred_element_type=jnp.float32
    ).reshape(rows, entry_count * BLK)
    projected = picked[:6]
    colours = picked[6:]
    cotangent = pix_grad.reshape(channels, TPD, -1).astype(jnp.float32)
    picture, grad_proj, grad_colour = tile_grads_direct(projected, colours, cotangent)
    entry_grads = jnp.concatenate([grad_proj, grad_colour], axis=0).astype(jnp.bfloat16)
    back = jnp.einsum(
        "reb,se->rbs",
        entry_grads.reshape(rows, entry_count, BLK),
        slot_hot,
        preferred_element_type=jnp.float32,
    ).astype(jnp.bfloat16)
    returned = lax.all_to_all(back, "tiles", split_axis=2, concat_axis=2, tiled=True)
    summed = jnp.einsum("rbs,ks->rbk", returned, owner_hot, preferred_element_type=jnp.float32)
    column_geometry = project_pullback(geometry_col, linear, summed[:6])
    column_colour = summed[6:]
    column_all = jnp.concatenate([column_geometry, column_colour], axis=0)
    grads = lax.all_to_all(
        column_all.reshape(rows, BLK, cams, local_blocks), "cams", 2, 2, tiled=True
    ).sum(axis=2)
    grads = grads.transpose(0, 2, 1).reshape(rows, local_blocks * BLK)
    grad_geometry = grads[:6]
    grad_appearance = grads[6:]
    return (picture.reshape(channels, 1, -1), grad_geometry, grad_appearance)


def solution(mesh):
    return jax.shard_map(
        local,
        mesh=mesh,
        in_specs=(
            P(None, ("tiles", "cams")),
            P(None, ("tiles", "cams")),
            P(("tiles", "cams")),
            P(("tiles", "cams")),
            P(None, ("tiles", "cams")),
            P("cams", None),
            P("cams", None),
            P("cams", "tiles", None, None),
            P(None, "cams", "tiles"),
        ),
        out_specs=(
            P(None, "cams", "tiles"),
            P(None, ("tiles", "cams")),
            P(None, ("tiles", "cams")),
        ),
        check_vma=False,
    )
```

```python
import jax
import jax.numpy as jnp
from jax import lax
from jax.sharding import PartitionSpec as P

SIDE = 16
TPD = 16
LIST = 3
BLK = 8


def project(geometry, linear, camera_shift):
    lin_xx = 1.0 + linear[0]
    lin_xy = linear[1]
    lin_yx = linear[2]
    lin_yy = 1.0 + linear[3]
    diag_x = geometry[2]
    diag_y = geometry[3]
    lower = geometry[4]
    cov_xx = diag_x * diag_x
    cov_xy = diag_x * lower
    cov_yy = lower * lower + diag_y * diag_y
    half_xx = lin_xx * cov_xx + lin_xy * cov_xy
    half_xy = lin_xx * cov_xy + lin_xy * cov_yy
    half_yx = lin_yx * cov_xx + lin_yy * cov_xy
    half_yy = lin_yx * cov_xy + lin_yy * cov_yy
    img_xx = half_xx * lin_xx + half_xy * lin_xy + 0.3
    img_xy = half_xx * lin_yx + half_xy * lin_yy
    img_yy = half_yx * lin_yx + half_yy * lin_yy + 0.3
    determ = img_xx * img_yy - img_xy * img_xy
    centre_x = lin_xx * geometry[0] + lin_xy * geometry[1] + camera_shift[0]
    centre_y = lin_yx * geometry[0] + lin_yy * geometry[1] + camera_shift[1]
    opacity = 0.95 * jax.nn.sigmoid(geometry[5])
    return jnp.stack(
        [centre_x, centre_y, img_yy / determ, -img_xy / determ, img_xx / determ, opacity]
    )


def project_pullback(geometry, linear, grad):
    lin_xx = 1.0 + linear[0]
    lin_xy = linear[1]
    lin_yx = linear[2]
    lin_yy = 1.0 + linear[3]
    diag_x = geometry[2]
    diag_y = geometry[3]
    lower = geometry[4]
    cov_xx = diag_x * diag_x
    cov_xy = diag_x * lower
    cov_yy = lower * lower + diag_y * diag_y
    half_xx = lin_xx * cov_xx + lin_xy * cov_xy
    half_xy = lin_xx * cov_xy + lin_xy * cov_yy
    half_yx = lin_yx * cov_xx + lin_yy * cov_xy
    half_yy = lin_yx * cov_xy + lin_yy * cov_yy
    img_xx = half_xx * lin_xx + half_xy * lin_xy + 0.3
    img_xy = half_xx * lin_yx + half_xy * lin_yy
    img_yy = half_yx * lin_yx + half_yy * lin_yy + 0.3
    determ = img_xx * img_yy - img_xy * img_xy
    inv = 1.0 / determ
    scale = (grad[2] * img_yy - grad[3] * img_xy + grad[4] * img_xx) * inv * inv
    g_xx = grad[4] * inv - scale * img_yy
    g_yy = grad[2] * inv - scale * img_xx
    g_xy = 2.0 * scale * img_xy - grad[3] * inv
    g_half_xx = g_xx * lin_xx + g_xy * lin_yx
    g_half_xy = g_xx * lin_xy + g_xy * lin_yy
    g_half_yx = g_yy * lin_yx
    g_half_yy = g_yy * lin_yy
    g_cov_xx = g_half_xx * lin_xx + g_half_yx * lin_yx
    g_cov_xy = g_half_xx * lin_xy + g_half_xy * lin_xx + g_half_yx * lin_yy + g_half_yy * lin_yx
    g_cov_yy = g_half_xy * lin_xy + g_half_yy * lin_yy
    opacity = jax.nn.sigmoid(geometry[5])
    return jnp.stack(
        [
            grad[0] * lin_xx + grad[1] * lin_yx,
            grad[0] * lin_xy + grad[1] * lin_yy,
            2.0 * g_cov_xx * diag_x + g_cov_xy * lower,
            2.0 * g_cov_yy * diag_y,
            g_cov_xy * diag_x + 2.0 * g_cov_yy * lower,
            grad[5] * 0.95 * opacity * (1.0 - opacity),
        ]
    )


def render_tile(projected, colours):
    pixels = jnp.arange(SIDE * SIDE)
    across = (pixels % SIDE).astype(jnp.float32) + 0.5 - SIDE / 2
    downward = (pixels // SIDE).astype(jnp.float32) + 0.5 - SIDE / 2
    delta_x = across[None, :] - projected[0][:, None]
    delta_y = downward[None, :] - projected[1][:, None]
    quadric = (
        projected[2][:, None] * delta_x * delta_x
        + 2.0 * projected[3][:, None] * delta_x * delta_y
        + projected[4][:, None] * delta_y * delta_y
    )
    coverage = projected[5][:, None] * jnp.exp(-0.5 * quadric)
    log_keep = jnp.log1p(-coverage)
    weight = jnp.exp(jnp.cumsum(log_keep, axis=0) - log_keep) * coverage
    return jnp.dot(
        colours, weight, precision=lax.Precision.HIGHEST, preferred_element_type=jnp.float32
    )


def tile_grads(projected, colours, cotangent):
    per_tile = projected.shape[1] // TPD
    channels = colours.shape[0]
    proj_tiles = projected.reshape(6, TPD, per_tile)
    colour_tiles = colours.reshape(channels, TPD, per_tile)

    def forward(proj_arg, colour_arg):
        return jax.vmap(render_tile, in_axes=(1, 1), out_axes=1)(proj_arg, colour_arg)

    picture, pullback = jax.vjp(forward, proj_tiles, colour_tiles)
    grad_proj, grad_colour = pullback(cotangent)
    return (picture, grad_proj.reshape(6, -1), grad_colour.reshape(channels, -1))


def slot_ranks(entries, blocks_per_column, columns):
    column = entries // blocks_per_column
    in_column = entries % blocks_per_column
    matches = (column[..., None] == jnp.arange(columns, dtype=jnp.int32)).astype(jnp.int32)
    before = jnp.cumsum(matches, axis=-2) - matches
    ranking = jnp.sum(before * matches, axis=-1)
    return (column, ranking, in_column)


def local(
    offsets,
    factor_diag,
    factor_off,
    logit,
    appearance,
    cam_linear,
    cam_shift,
    block_lists,
    pix_grad,
):
    columns = lax.axis_size("tiles")
    capacity = 4 * TPD * LIST // columns
    slot_count = columns * capacity
    channels = appearance.shape[0]
    geometry = jnp.concatenate([offsets, factor_diag, factor_off[None, :], logit[None, :]], axis=0)
    params = jnp.concatenate([geometry, appearance], axis=0)
    cams = lax.axis_size("cams")
    local_blocks = params.shape[1] // BLK
    per_column = cams * local_blocks
    by_lane = params.reshape(params.shape[0], local_blocks, BLK).transpose(0, 2, 1)
    gathered = lax.all_to_all(
        jnp.broadcast_to(by_lane[None], (cams,) + by_lane.shape), "cams", 0, 0, tiled=True
    )
    params_col = gathered.transpose(1, 2, 0, 3).reshape(params.shape[0], BLK, per_column)
    linear = cam_linear[0]
    camera_shift = cam_shift[0]
    entries = block_lists.reshape(-1)
    entry_count = entries.shape[0]
    column, ranking, in_column = slot_ranks(entries, per_column, columns)
    entry_slot = column * capacity + ranking
    request = jnp.zeros((slot_count,), jnp.int32).at[entry_slot].set(in_column)
    request, params_col = lax.optimization_barrier((request, params_col))
    geometry_col = params_col[:6]
    appearance_col = params_col[6:]
    wanted = lax.all_to_all(request, "tiles", split_axis=0, concat_axis=0, tiled=True)
    rows = params_col.shape[0]
    payload_col = jnp.concatenate(
        [project(geometry_col, linear, camera_shift), appearance_col], axis=0
    ).astype(jnp.bfloat16)
    owner_hot = (jnp.arange(per_column, dtype=jnp.int32)[:, None] == wanted[None, :]).astype(
        jnp.bfloat16
    )
    send = jnp.einsum(
        "rbk,ks->rbs",
        payload_col,
        owner_hot,
        preferred_element_type=jnp.float32,
    ).astype(jnp.bfloat16)
    sent = lax.all_to_all(send, "tiles", split_axis=2, concat_axis=2, tiled=True)
    slot_hot = (jnp.arange(slot_count, dtype=jnp.int32)[:, None] == entry_slot[None, :]).astype(
        jnp.bfloat16
    )
    picked = jnp.einsum(
        "rbs,se->reb", sent, slot_hot, preferred_element_type=jnp.float32
    ).reshape(rows, entry_count * BLK)
    projected = picked[:6]
    colours = picked[6:]
    cotangent = pix_grad.reshape(channels, TPD, -1).astype(jnp.float32)
    picture, grad_proj, grad_colour = tile_grads(projected, colours, cotangent)
    entry_grads = jnp.concatenate([grad_proj, grad_colour], axis=0).astype(jnp.bfloat16)
    back = jnp.einsum(
        "reb,se->rbs",
        entry_grads.reshape(rows, entry_count, BLK),
        slot_hot,
        preferred_element_type=jnp.float32,
    ).astype(jnp.bfloat16)
    returned = lax.all_to_all(back, "tiles", split_axis=2, concat_axis=2, tiled=True)
    summed = jnp.einsum("rbs,ks->rbk", returned, owner_hot, preferred_element_type=jnp.float32)
    column_geometry = project_pullback(geometry_col, linear, summed[:6])
    column_colour = summed[6:]
    column_all = jnp.concatenate([column_geometry, column_colour], axis=0)
    grads = lax.all_to_all(
        column_all.reshape(rows, BLK, cams, local_blocks), "cams", 2, 2, tiled=True
    )

    def finish(part):
        return part.sum(axis=2).transpose(0, 2, 1).reshape(part.shape[0], local_blocks * BLK)

    grad_geometry = finish(grads[:6])
    grad_appearance = finish(grads[6:])
    return (picture.reshape(channels, 1, -1), grad_geometry, grad_appearance)


def solution(mesh):
    return jax.shard_map(
        local,
        mesh=mesh,
        in_specs=(
            P(None, ("tiles", "cams")),
            P(None, ("tiles", "cams")),
            P(("tiles", "cams")),
            P(("tiles", "cams")),
            P(None, ("tiles", "cams")),
            P("cams", None),
            P("cams", None),
            P("cams", "tiles", None, None),
            P(None, "cams", "tiles"),
        ),
        out_specs=(
            P(None, "cams", "tiles"),
            P(None, ("tiles", "cams")),
            P(None, ("tiles", "cams")),
        ),
        check_vma=False,
    )
```

```python
import jax
import jax.numpy as jnp
from jax import lax
from jax.sharding import PartitionSpec as P

SIDE = 16
TPD = 16
LIST = 3
BLK = 8


def project(geometry, linear, camera_shift):
    lin_xx = 1.0 + linear[0]
    lin_xy = linear[1]
    lin_yx = linear[2]
    lin_yy = 1.0 + linear[3]
    diag_x = geometry[2]
    diag_y = geometry[3]
    lower = geometry[4]
    cov_xx = diag_x * diag_x
    cov_xy = diag_x * lower
    cov_yy = lower * lower + diag_y * diag_y
    half_xx = lin_xx * cov_xx + lin_xy * cov_xy
    half_xy = lin_xx * cov_xy + lin_xy * cov_yy
    half_yx = lin_yx * cov_xx + lin_yy * cov_xy
    half_yy = lin_yx * cov_xy + lin_yy * cov_yy
    img_xx = half_xx * lin_xx + half_xy * lin_xy + 0.3
    img_xy = half_xx * lin_yx + half_xy * lin_yy
    img_yy = half_yx * lin_yx + half_yy * lin_yy + 0.3
    determ = img_xx * img_yy - img_xy * img_xy
    centre_x = lin_xx * geometry[0] + lin_xy * geometry[1] + camera_shift[0]
    centre_y = lin_yx * geometry[0] + lin_yy * geometry[1] + camera_shift[1]
    opacity = 0.95 * jax.nn.sigmoid(geometry[5])
    return jnp.stack(
        [centre_x, centre_y, img_yy / determ, -img_xy / determ, img_xx / determ, opacity]
    )


def project_pullback(geometry, linear, grad):
    lin_xx = 1.0 + linear[0]
    lin_xy = linear[1]
    lin_yx = linear[2]
    lin_yy = 1.0 + linear[3]
    diag_x = geometry[2]
    diag_y = geometry[3]
    lower = geometry[4]
    cov_xx = diag_x * diag_x
    cov_xy = diag_x * lower
    cov_yy = lower * lower + diag_y * diag_y
    half_xx = lin_xx * cov_xx + lin_xy * cov_xy
    half_xy = lin_xx * cov_xy + lin_xy * cov_yy
    half_yx = lin_yx * cov_xx + lin_yy * cov_xy
    half_yy = lin_yx * cov_xy + lin_yy * cov_yy
    img_xx = half_xx * lin_xx + half_xy * lin_xy + 0.3
    img_xy = half_xx * lin_yx + half_xy * lin_yy
    img_yy = half_yx * lin_yx + half_yy * lin_yy + 0.3
    determ = img_xx * img_yy - img_xy * img_xy
    inv = 1.0 / determ
    scale = (grad[2] * img_yy - grad[3] * img_xy + grad[4] * img_xx) * inv * inv
    g_xx = grad[4] * inv - scale * img_yy
    g_yy = grad[2] * inv - scale * img_xx
    g_xy = 2.0 * scale * img_xy - grad[3] * inv
    g_half_xx = g_xx * lin_xx + g_xy * lin_yx
    g_half_xy = g_xx * lin_xy + g_xy * lin_yy
    g_half_yx = g_yy * lin_yx
    g_half_yy = g_yy * lin_yy
    g_cov_xx = g_half_xx * lin_xx + g_half_yx * lin_yx
    g_cov_xy = g_half_xx * lin_xy + g_half_xy * lin_xx + g_half_yx * lin_yy + g_half_yy * lin_yx
    g_cov_yy = g_half_xy * lin_xy + g_half_yy * lin_yy
    opacity = jax.nn.sigmoid(geometry[5])
    return jnp.stack(
        [
            grad[0] * lin_xx + grad[1] * lin_yx,
            grad[0] * lin_xy + grad[1] * lin_yy,
            2.0 * g_cov_xx * diag_x + g_cov_xy * lower,
            2.0 * g_cov_yy * diag_y,
            g_cov_xy * diag_x + 2.0 * g_cov_yy * lower,
            grad[5] * 0.95 * opacity * (1.0 - opacity),
        ]
    )


def render_tile(projected, colours):
    pixels = jnp.arange(SIDE * SIDE)
    across = (pixels % SIDE).astype(jnp.float32) + 0.5 - SIDE / 2
    downward = (pixels // SIDE).astype(jnp.float32) + 0.5 - SIDE / 2
    delta_x = across[None, :] - projected[0][:, None]
    delta_y = downward[None, :] - projected[1][:, None]
    quadric = (
        projected[2][:, None] * delta_x * delta_x
        + 2.0 * projected[3][:, None] * delta_x * delta_y
        + projected[4][:, None] * delta_y * delta_y
    )
    coverage = projected[5][:, None] * jnp.exp(-0.5 * quadric)
    log_keep = jnp.log1p(-coverage)
    weight = jnp.exp(jnp.cumsum(log_keep, axis=0) - log_keep) * coverage
    return jnp.dot(
        colours, weight, precision=lax.Precision.HIGHEST, preferred_element_type=jnp.float32
    )


def tile_grads(projected, colours, cotangent):
    per_tile = projected.shape[1] // TPD
    channels = colours.shape[0]
    proj_tiles = projected.reshape(6, TPD, per_tile)
    colour_tiles = colours.reshape(channels, TPD, per_tile)

    def forward(proj_arg, colour_arg):
        return jax.vmap(render_tile, in_axes=(1, 1), out_axes=1)(proj_arg, colour_arg)

    picture, pullback = jax.vjp(forward, proj_tiles, colour_tiles)
    grad_proj, grad_colour = pullback(cotangent)
    return (picture, grad_proj.reshape(6, -1), grad_colour.reshape(channels, -1))


def slot_ranks(entries, blocks_per_column, columns):
    column = entries // blocks_per_column
    in_column = entries % blocks_per_column
    matches = (column[..., None] == jnp.arange(columns, dtype=jnp.int32)).astype(jnp.int32)
    before = jnp.cumsum(matches, axis=-2) - matches
    ranking = jnp.sum(before * matches, axis=-1)
    return (column, ranking, in_column)


def local(
    offsets,
    factor_diag,
    factor_off,
    logit,
    appearance,
    cam_linear,
    cam_shift,
    block_lists,
    pix_grad,
):
    columns = lax.axis_size("tiles")
    capacity = 4 * TPD * LIST // columns
    slot_count = columns * capacity
    channels = appearance.shape[0]
    geometry = jnp.concatenate([offsets, factor_diag, factor_off[None, :], logit[None, :]], axis=0)
    params = jnp.concatenate([geometry, appearance], axis=0)
    cams = lax.axis_size("cams")
    local_blocks = params.shape[1] // BLK
    per_column = cams * local_blocks
    by_lane = params.reshape(params.shape[0], local_blocks, BLK).transpose(0, 2, 1)
    gathered = lax.all_to_all(
        jnp.broadcast_to(by_lane[None], (cams,) + by_lane.shape), "cams", 0, 0, tiled=True
    )
    params_col = gathered.transpose(1, 2, 0, 3).reshape(params.shape[0], BLK, per_column)
    linear = cam_linear[0]
    camera_shift = cam_shift[0]
    entries = block_lists.reshape(-1)
    entry_count = entries.shape[0]
    column, ranking, in_column = slot_ranks(entries, per_column, columns)
    entry_slot = column * capacity + ranking
    request = jnp.zeros((slot_count,), jnp.int32).at[entry_slot].set(in_column)
    request, params_col = lax.optimization_barrier((request, params_col))
    geometry_col = params_col[:6]
    appearance_col = params_col[6:]
    wanted = lax.all_to_all(request, "tiles", split_axis=0, concat_axis=0, tiled=True)
    rows = params_col.shape[0]
    payload_col = jnp.concatenate(
        [project(geometry_col, linear, camera_shift), appearance_col], axis=0
    ).astype(jnp.bfloat16)
    owner_hot = (jnp.arange(per_column, dtype=jnp.int32)[:, None] == wanted[None, :]).astype(
        jnp.bfloat16
    )
    send = jnp.einsum(
        "rbk,ks->rbs",
        payload_col,
        owner_hot,
        preferred_element_type=jnp.float32,
    ).astype(jnp.bfloat16)
    sent = lax.all_to_all(send, "tiles", split_axis=2, concat_axis=2, tiled=True)
    slot_hot = (jnp.arange(slot_count, dtype=jnp.int32)[:, None] == entry_slot[None, :]).astype(
        jnp.bfloat16
    )
    picked = jnp.einsum(
        "rbs,se->reb", sent, slot_hot, preferred_element_type=jnp.float32
    ).reshape(rows, entry_count * BLK)
    projected = picked[:6]
    colours = picked[6:]
    cotangent = pix_grad.reshape(channels, TPD, -1).astype(jnp.float32)
    picture, grad_proj, grad_colour = tile_grads(projected, colours, cotangent)
    entry_grads = jnp.concatenate([grad_proj, grad_colour], axis=0).astype(jnp.bfloat16)
    back = jnp.einsum(
        "reb,se->rbs",
        entry_grads.reshape(rows, entry_count, BLK),
        slot_hot,
        preferred_element_type=jnp.float32,
    ).astype(jnp.bfloat16)
    unit = jnp.eye(6, dtype=jnp.float32)[:, :, None, None]
    ones = jnp.ones_like(geometry_col[0])
    coeffs = jnp.stack(
        [project_pullback(geometry_col, linear, unit[k] * ones)[2:5] for k in (2, 3, 4)]
    )
    slope = project_pullback(geometry_col, linear, unit[5] * ones)[5]
    back, coeffs, slope = lax.optimization_barrier((back, coeffs, slope))
    returned = lax.all_to_all(back, "tiles", split_axis=2, concat_axis=2, tiled=True)
    summed = jnp.einsum("rbs,ks->rbk", returned, owner_hot, preferred_element_type=jnp.float32)
    lin_xx = 1.0 + linear[0]
    lin_yy = 1.0 + linear[3]
    conic_rows = coeffs[0] * summed[2] + coeffs[1] * summed[3] + coeffs[2] * summed[4]
    column_geometry = jnp.concatenate(
        [
            jnp.stack(
                [
                    summed[0] * lin_xx + summed[1] * linear[2],
                    summed[0] * linear[1] + summed[1] * lin_yy,
                ]
            ),
            conic_rows,
            (summed[5] * slope)[None],
        ],
        axis=0,
    )
    column_colour = summed[6:]
    column_all = jnp.concatenate([column_geometry, column_colour], axis=0)
    grads = lax.all_to_all(
        column_all.reshape(rows, BLK, cams, local_blocks), "cams", 2, 2, tiled=True
    ).sum(axis=2)
    grads = grads.transpose(0, 2, 1).reshape(rows, local_blocks * BLK)
    grad_geometry = grads[:6]
    grad_appearance = grads[6:]
    return (picture.reshape(channels, 1, -1), grad_geometry, grad_appearance)


def solution(mesh):
    return jax.shard_map(
        local,
        mesh=mesh,
        in_specs=(
            P(None, ("tiles", "cams")),
            P(None, ("tiles", "cams")),
            P(("tiles", "cams")),
            P(("tiles", "cams")),
            P(None, ("tiles", "cams")),
            P("cams", None),
            P("cams", None),
            P("cams", "tiles", None, None),
            P(None, "cams", "tiles"),
        ),
        out_specs=(
            P(None, "cams", "tiles"),
            P(None, ("tiles", "cams")),
            P(None, ("tiles", "cams")),
        ),
        check_vma=False,
    )
```

```python
import jax
import jax.numpy as jnp
from jax import lax
from jax.sharding import PartitionSpec as P

SIDE = 16
TPD = 16
LIST = 3
BLK = 8


def project(geometry, linear, camera_shift):
    lin_xx = 1.0 + linear[0]
    lin_xy = linear[1]
    lin_yx = linear[2]
    lin_yy = 1.0 + linear[3]
    diag_x = geometry[2]
    diag_y = geometry[3]
    lower = geometry[4]
    cov_xx = diag_x * diag_x
    cov_xy = diag_x * lower
    cov_yy = lower * lower + diag_y * diag_y
    half_xx = lin_xx * cov_xx + lin_xy * cov_xy
    half_xy = lin_xx * cov_xy + lin_xy * cov_yy
    half_yx = lin_yx * cov_xx + lin_yy * cov_xy
    half_yy = lin_yx * cov_xy + lin_yy * cov_yy
    img_xx = half_xx * lin_xx + half_xy * lin_xy + 0.3
    img_xy = half_xx * lin_yx + half_xy * lin_yy
    img_yy = half_yx * lin_yx + half_yy * lin_yy + 0.3
    determ = img_xx * img_yy - img_xy * img_xy
    centre_x = lin_xx * geometry[0] + lin_xy * geometry[1] + camera_shift[0]
    centre_y = lin_yx * geometry[0] + lin_yy * geometry[1] + camera_shift[1]
    opacity = 0.95 * jax.nn.sigmoid(geometry[5])
    return jnp.stack(
        [centre_x, centre_y, img_yy / determ, -img_xy / determ, img_xx / determ, opacity]
    )


def project_pullback(geometry, linear, grad):
    lin_xx = 1.0 + linear[0]
    lin_xy = linear[1]
    lin_yx = linear[2]
    lin_yy = 1.0 + linear[3]
    diag_x = geometry[2]
    diag_y = geometry[3]
    lower = geometry[4]
    cov_xx = diag_x * diag_x
    cov_xy = diag_x * lower
    cov_yy = lower * lower + diag_y * diag_y
    half_xx = lin_xx * cov_xx + lin_xy * cov_xy
    half_xy = lin_xx * cov_xy + lin_xy * cov_yy
    half_yx = lin_yx * cov_xx + lin_yy * cov_xy
    half_yy = lin_yx * cov_xy + lin_yy * cov_yy
    img_xx = half_xx * lin_xx + half_xy * lin_xy + 0.3
    img_xy = half_xx * lin_yx + half_xy * lin_yy
    img_yy = half_yx * lin_yx + half_yy * lin_yy + 0.3
    determ = img_xx * img_yy - img_xy * img_xy
    inv = 1.0 / determ
    scale = (grad[2] * img_yy - grad[3] * img_xy + grad[4] * img_xx) * inv * inv
    g_xx = grad[4] * inv - scale * img_yy
    g_yy = grad[2] * inv - scale * img_xx
    g_xy = 2.0 * scale * img_xy - grad[3] * inv
    g_half_xx = g_xx * lin_xx + g_xy * lin_yx
    g_half_xy = g_xx * lin_xy + g_xy * lin_yy
    g_half_yx = g_yy * lin_yx
    g_half_yy = g_yy * lin_yy
    g_cov_xx = g_half_xx * lin_xx + g_half_yx * lin_yx
    g_cov_xy = g_half_xx * lin_xy + g_half_xy * lin_xx + g_half_yx * lin_yy + g_half_yy * lin_yx
    g_cov_yy = g_half_xy * lin_xy + g_half_yy * lin_yy
    opacity = jax.nn.sigmoid(geometry[5])
    return jnp.stack(
        [
            grad[0] * lin_xx + grad[1] * lin_yx,
            grad[0] * lin_xy + grad[1] * lin_yy,
            2.0 * g_cov_xx * diag_x + g_cov_xy * lower,
            2.0 * g_cov_yy * diag_y,
            g_cov_xy * diag_x + 2.0 * g_cov_yy * lower,
            grad[5] * 0.95 * opacity * (1.0 - opacity),
        ]
    )


def render_tile(projected, colours):
    pixels = jnp.arange(SIDE * SIDE)
    across = (pixels % SIDE).astype(jnp.float32) + 0.5 - SIDE / 2
    downward = (pixels // SIDE).astype(jnp.float32) + 0.5 - SIDE / 2
    delta_x = across[None, :] - projected[0][:, None]
    delta_y = downward[None, :] - projected[1][:, None]
    quadric = (
        projected[2][:, None] * delta_x * delta_x
        + 2.0 * projected[3][:, None] * delta_x * delta_y
        + projected[4][:, None] * delta_y * delta_y
    )
    coverage = projected[5][:, None] * jnp.exp(-0.5 * quadric)
    log_keep = jnp.log1p(-coverage)
    weight = jnp.exp(jnp.cumsum(log_keep, axis=0) - log_keep) * coverage
    return jnp.dot(
        colours, weight, precision=lax.Precision.HIGHEST, preferred_element_type=jnp.float32
    )


def tile_grads(projected, colours, cotangent):
    per_tile = projected.shape[1] // TPD
    channels = colours.shape[0]
    proj_tiles = projected.reshape(6, TPD, per_tile)
    colour_tiles = colours.reshape(channels, TPD, per_tile)

    def forward(proj_arg, colour_arg):
        return jax.vmap(render_tile, in_axes=(1, 1), out_axes=1)(proj_arg, colour_arg)

    picture, pullback = jax.vjp(forward, proj_tiles, colour_tiles)
    grad_proj, grad_colour = pullback(cotangent)
    return (picture, grad_proj.reshape(6, -1), grad_colour.reshape(channels, -1))


def tile_grads_direct(projected, colours, cotangent):
    channels = colours.shape[0]
    proj = projected.reshape(6, TPD, -1)
    colour_tiles = colours.reshape(channels, TPD, -1)
    pixels = jnp.arange(SIDE * SIDE)
    across = (pixels % SIDE).astype(jnp.float32) + 0.5 - SIDE / 2
    downward = (pixels // SIDE).astype(jnp.float32) + 0.5 - SIDE / 2
    delta_x = across[None, None, :] - proj[0][..., None]
    delta_y = downward[None, None, :] - proj[1][..., None]
    conic_0 = proj[2][..., None]
    conic_1 = proj[3][..., None]
    conic_2 = proj[4][..., None]
    quadric = (
        conic_0 * delta_x * delta_x
        + 2.0 * conic_1 * delta_x * delta_y
        + conic_2 * delta_y * delta_y
    )
    falloff = jnp.exp(-0.5 * quadric)
    coverage = proj[5][..., None] * falloff
    log_keep = jnp.log1p(-coverage)
    keep = jnp.exp(jnp.cumsum(log_keep, axis=1) - log_keep)
    weight = keep * coverage
    hi = lax.Precision.HIGHEST
    picture = jnp.einsum("cti,tip->ctp", colour_tiles, weight, precision=hi)
    grad_colour = jnp.einsum("ctp,tip->cti", cotangent, weight, precision=hi)
    grad_weight = jnp.einsum("cti,ctp->tip", colour_tiles, cotangent, precision=hi)
    grad_sum = grad_weight * weight
    grad_log = jnp.sum(grad_sum, axis=1, keepdims=True) - jnp.cumsum(grad_sum, axis=1)
    grad_cover = grad_weight * keep - grad_log / (1.0 - coverage)
    grad_quad = -0.5 * grad_cover * coverage
    basis = jnp.stack(
        [
            jnp.ones_like(across),
            across,
            downward,
            across * across,
            across * downward,
            downward * downward,
        ],
        axis=1,
    )
    moments = jnp.einsum(
        "tip,pk->tik",
        jnp.concatenate([grad_quad, grad_cover * falloff], axis=1),
        basis,
        precision=hi,
    )
    count = grad_quad.shape[1]
    m_1, m_x, m_y, m_xx, m_xy, m_yy = [moments[:, :count, k] for k in range(6)]
    centre_x = proj[0]
    centre_y = proj[1]
    s_x = m_x - centre_x * m_1
    s_y = m_y - centre_y * m_1
    s_xx = m_xx - 2.0 * centre_x * m_x + centre_x * centre_x * m_1
    s_xy = m_xy - centre_x * m_y - centre_y * m_x + centre_x * centre_y * m_1
    s_yy = m_yy - 2.0 * centre_y * m_y + centre_y * centre_y * m_1
    grad_proj = jnp.stack(
        [
            -2.0 * (proj[2] * s_x + proj[3] * s_y),
            -2.0 * (proj[3] * s_x + proj[4] * s_y),
            s_xx,
            2.0 * s_xy,
            s_yy,
            moments[:, count:, 0],
        ]
    )
    return (picture, grad_proj.reshape(6, -1), grad_colour.reshape(channels, -1))


def slot_ranks(entries, blocks_per_column, columns):
    column = entries // blocks_per_column
    in_column = entries % blocks_per_column
    matches = (column[..., None] == jnp.arange(columns, dtype=jnp.int32)).astype(jnp.int32)
    before = jnp.cumsum(matches, axis=-2) - matches
    ranking = jnp.sum(before * matches, axis=-1)
    return (column, ranking, in_column)


def local(
    offsets,
    factor_diag,
    factor_off,
    logit,
    appearance,
    cam_linear,
    cam_shift,
    block_lists,
    pix_grad,
):
    columns = lax.axis_size("tiles")
    capacity = 4 * TPD * LIST // columns
    slot_count = columns * capacity
    channels = appearance.shape[0]
    geometry = jnp.concatenate([offsets, factor_diag, factor_off[None, :], logit[None, :]], axis=0)
    params = jnp.concatenate([geometry, appearance], axis=0)
    cams = lax.axis_size("cams")
    local_blocks = params.shape[1] // BLK
    per_column = cams * local_blocks
    by_lane = params.reshape(params.shape[0], local_blocks, BLK).transpose(0, 2, 1)
    gathered = lax.all_to_all(
        jnp.broadcast_to(by_lane[None], (cams,) + by_lane.shape), "cams", 0, 0, tiled=True
    )
    params_col = gathered.transpose(1, 2, 0, 3).reshape(params.shape[0], BLK, per_column)
    linear = cam_linear[0]
    camera_shift = cam_shift[0]
    entries = block_lists.reshape(-1)
    entry_count = entries.shape[0]
    column, ranking, in_column = slot_ranks(entries, per_column, columns)
    entry_slot = column * capacity + ranking
    request = jnp.zeros((slot_count,), jnp.int32).at[entry_slot].set(in_column)
    request, params_col = lax.optimization_barrier((request, params_col))
    geometry_col = params_col[:6]
    appearance_col = params_col[6:]
    wanted = lax.all_to_all(request, "tiles", split_axis=0, concat_axis=0, tiled=True)
    rows = params_col.shape[0]
    payload_col = jnp.concatenate(
        [project(geometry_col, linear, camera_shift), appearance_col], axis=0
    ).astype(jnp.bfloat16)
    owner_hot = (jnp.arange(per_column, dtype=jnp.int32)[:, None] == wanted[None, :]).astype(
        jnp.bfloat16
    )
    send = jnp.einsum(
        "rbk,ks->rbs",
        payload_col,
        owner_hot,
        preferred_element_type=jnp.float32,
    ).astype(jnp.bfloat16)
    sent = lax.all_to_all(send, "tiles", split_axis=2, concat_axis=2, tiled=True)
    slot_hot = (jnp.arange(slot_count, dtype=jnp.int32)[:, None] == entry_slot[None, :]).astype(
        jnp.bfloat16
    )
    picked = jnp.einsum(
        "rbs,se->reb", sent, slot_hot, preferred_element_type=jnp.float32
    ).reshape(rows, entry_count * BLK)
    projected = picked[:6]
    colours = picked[6:]
    cotangent = pix_grad.reshape(channels, TPD, -1).astype(jnp.float32)
    picture, grad_proj, grad_colour = tile_grads_direct(projected, colours, cotangent)
    entry_grads = jnp.concatenate([grad_proj, grad_colour], axis=0).astype(jnp.bfloat16)
    back = jnp.einsum(
        "reb,se->rbs",
        entry_grads.reshape(rows, entry_count, BLK),
        slot_hot,
        preferred_element_type=jnp.float32,
    ).astype(jnp.bfloat16)
    returned = lax.all_to_all(back, "tiles", split_axis=2, concat_axis=2, tiled=True)
    summed = jnp.einsum("rbs,ks->rbk", returned, owner_hot, preferred_element_type=jnp.float32)
    column_geometry = project_pullback(geometry_col, linear, summed[:6])
    column_colour = summed[6:]
    column_all = jnp.concatenate([column_geometry, column_colour], axis=0)
    grads = lax.all_to_all(
        column_all.reshape(rows, BLK, cams, local_blocks), "cams", 2, 2, tiled=True
    ).sum(axis=2)
    grads = grads.transpose(0, 2, 1).reshape(rows, local_blocks * BLK)
    grad_geometry = grads[:6]
    grad_appearance = grads[6:]
    return (picture.reshape(channels, 1, -1), grad_geometry, grad_appearance)


def solution(mesh):
    return jax.shard_map(
        local,
        mesh=mesh,
        in_specs=(
            P(None, ("tiles", "cams")),
            P(None, ("tiles", "cams")),
            P(("tiles", "cams")),
            P(("tiles", "cams")),
            P(None, ("tiles", "cams")),
            P("cams", None),
            P("cams", None),
            P("cams", "tiles", None, None),
            P(None, "cams", "tiles"),
        ),
        out_specs=(
            P(None, "cams", "tiles"),
            P(None, ("tiles", "cams")),
            P(None, ("tiles", "cams")),
        ),
        check_vma=False,
    )
```

```python
import jax
import jax.numpy as jnp
from jax import lax
from jax.sharding import PartitionSpec as P

SIDE = 16
TPD = 16
LIST = 3
BLK = 8


def project(geometry, linear, camera_shift):
    lin_xx = 1.0 + linear[0]
    lin_xy = linear[1]
    lin_yx = linear[2]
    lin_yy = 1.0 + linear[3]
    diag_x = geometry[2]
    diag_y = geometry[3]
    lower = geometry[4]
    cov_xx = diag_x * diag_x
    cov_xy = diag_x * lower
    cov_yy = lower * lower + diag_y * diag_y
    half_xx = lin_xx * cov_xx + lin_xy * cov_xy
    half_xy = lin_xx * cov_xy + lin_xy * cov_yy
    half_yx = lin_yx * cov_xx + lin_yy * cov_xy
    half_yy = lin_yx * cov_xy + lin_yy * cov_yy
    img_xx = half_xx * lin_xx + half_xy * lin_xy + 0.3
    img_xy = half_xx * lin_yx + half_xy * lin_yy
    img_yy = half_yx * lin_yx + half_yy * lin_yy + 0.3
    determ = img_xx * img_yy - img_xy * img_xy
    centre_x = lin_xx * geometry[0] + lin_xy * geometry[1] + camera_shift[0]
    centre_y = lin_yx * geometry[0] + lin_yy * geometry[1] + camera_shift[1]
    opacity = 0.95 * jax.nn.sigmoid(geometry[5])
    return jnp.stack(
        [centre_x, centre_y, img_yy / determ, -img_xy / determ, img_xx / determ, opacity]
    )


def project_pullback(geometry, linear, grad):
    lin_xx = 1.0 + linear[0]
    lin_xy = linear[1]
    lin_yx = linear[2]
    lin_yy = 1.0 + linear[3]
    diag_x = geometry[2]
    diag_y = geometry[3]
    lower = geometry[4]
    cov_xx = diag_x * diag_x
    cov_xy = diag_x * lower
    cov_yy = lower * lower + diag_y * diag_y
    half_xx = lin_xx * cov_xx + lin_xy * cov_xy
    half_xy = lin_xx * cov_xy + lin_xy * cov_yy
    half_yx = lin_yx * cov_xx + lin_yy * cov_xy
    half_yy = lin_yx * cov_xy + lin_yy * cov_yy
    img_xx = half_xx * lin_xx + half_xy * lin_xy + 0.3
    img_xy = half_xx * lin_yx + half_xy * lin_yy
    img_yy = half_yx * lin_yx + half_yy * lin_yy + 0.3
    determ = img_xx * img_yy - img_xy * img_xy
    inv = 1.0 / determ
    scale = (grad[2] * img_yy - grad[3] * img_xy + grad[4] * img_xx) * inv * inv
    g_xx = grad[4] * inv - scale * img_yy
    g_yy = grad[2] * inv - scale * img_xx
    g_xy = 2.0 * scale * img_xy - grad[3] * inv
    g_half_xx = g_xx * lin_xx + g_xy * lin_yx
    g_half_xy = g_xx * lin_xy + g_xy * lin_yy
    g_half_yx = g_yy * lin_yx
    g_half_yy = g_yy * lin_yy
    g_cov_xx = g_half_xx * lin_xx + g_half_yx * lin_yx
    g_cov_xy = g_half_xx * lin_xy + g_half_xy * lin_xx + g_half_yx * lin_yy + g_half_yy * lin_yx
    g_cov_yy = g_half_xy * lin_xy + g_half_yy * lin_yy
    opacity = jax.nn.sigmoid(geometry[5])
    return jnp.stack(
        [
            grad[0] * lin_xx + grad[1] * lin_yx,
            grad[0] * lin_xy + grad[1] * lin_yy,
            2.0 * g_cov_xx * diag_x + g_cov_xy * lower,
            2.0 * g_cov_yy * diag_y,
            g_cov_xy * diag_x + 2.0 * g_cov_yy * lower,
            grad[5] * 0.95 * opacity * (1.0 - opacity),
        ]
    )


def render_tile(projected, colours):
    pixels = jnp.arange(SIDE * SIDE)
    across = (pixels % SIDE).astype(jnp.float32) + 0.5 - SIDE / 2
    downward = (pixels // SIDE).astype(jnp.float32) + 0.5 - SIDE / 2
    delta_x = across[None, :] - projected[0][:, None]
    delta_y = downward[None, :] - projected[1][:, None]
    quadric = (
        projected[2][:, None] * delta_x * delta_x
        + 2.0 * projected[3][:, None] * delta_x * delta_y
        + projected[4][:, None] * delta_y * delta_y
    )
    coverage = projected[5][:, None] * jnp.exp(-0.5 * quadric)
    log_keep = jnp.log1p(-coverage)
    weight = jnp.exp(jnp.cumsum(log_keep, axis=0) - log_keep) * coverage
    return jnp.dot(
        colours, weight, precision=lax.Precision.HIGHEST, preferred_element_type=jnp.float32
    )


def tile_grads(projected, colours, cotangent):
    per_tile = projected.shape[1] // TPD
    channels = colours.shape[0]
    proj_tiles = projected.reshape(6, TPD, per_tile)
    colour_tiles = colours.reshape(channels, TPD, per_tile)

    def forward(proj_arg, colour_arg):
        return jax.vmap(render_tile, in_axes=(1, 1), out_axes=1)(proj_arg, colour_arg)

    picture, pullback = jax.vjp(forward, proj_tiles, colour_tiles)
    grad_proj, grad_colour = pullback(cotangent)
    return (picture, grad_proj.reshape(6, -1), grad_colour.reshape(channels, -1))


def slot_ranks(entries, blocks_per_column, columns):
    column = entries // blocks_per_column
    in_column = entries % blocks_per_column
    matches = (column[..., None] == jnp.arange(columns, dtype=jnp.int32)).astype(jnp.int32)
    before = jnp.cumsum(matches, axis=-2) - matches
    ranking = jnp.sum(before * matches, axis=-1)
    return (column, ranking, in_column)


def local(
    offsets,
    factor_diag,
    factor_off,
    logit,
    appearance,
    cam_linear,
    cam_shift,
    block_lists,
    pix_grad,
):
    columns = lax.axis_size("tiles")
    capacity = 4 * TPD * LIST // columns
    slot_count = columns * capacity
    channels = appearance.shape[0]
    geometry = jnp.concatenate([offsets, factor_diag, factor_off[None, :], logit[None, :]], axis=0)
    params = jnp.concatenate([geometry, appearance], axis=0)
    cams = lax.axis_size("cams")
    local_blocks = params.shape[1] // BLK
    per_column = cams * local_blocks
    by_lane = params.reshape(params.shape[0], local_blocks, BLK).transpose(0, 2, 1)
    flat = by_lane.reshape(1, -1)
    gathered = lax.all_to_all(
        jnp.broadcast_to(flat, (cams, flat.shape[1])), "cams", 0, 0, tiled=True
    ).reshape((cams,) + by_lane.shape)
    params_col = gathered.transpose(1, 2, 0, 3).reshape(params.shape[0], BLK, per_column)
    linear = cam_linear[0]
    camera_shift = cam_shift[0]
    entries = block_lists.reshape(-1)
    entry_count = entries.shape[0]
    column, ranking, in_column = slot_ranks(entries, per_column, columns)
    entry_slot = column * capacity + ranking
    request = jnp.zeros((slot_count,), jnp.int32).at[entry_slot].set(in_column)
    request, params_col = lax.optimization_barrier((request, params_col))
    geometry_col = params_col[:6]
    appearance_col = params_col[6:]
    wanted = lax.all_to_all(request, "tiles", split_axis=0, concat_axis=0, tiled=True)
    rows = params_col.shape[0]
    payload_col = jnp.concatenate(
        [project(geometry_col, linear, camera_shift), appearance_col], axis=0
    ).astype(jnp.bfloat16)
    owner_hot = (jnp.arange(per_column, dtype=jnp.int32)[:, None] == wanted[None, :]).astype(
        jnp.bfloat16
    )
    send = jnp.einsum(
        "rbk,ks->rbs",
        payload_col,
        owner_hot,
        preferred_element_type=jnp.float32,
    ).astype(jnp.bfloat16)
    sent = lax.all_to_all(send, "tiles", split_axis=2, concat_axis=2, tiled=True)
    slot_hot = (jnp.arange(slot_count, dtype=jnp.int32)[:, None] == entry_slot[None, :]).astype(
        jnp.bfloat16
    )
    picked = jnp.einsum(
        "rbs,se->reb", sent, slot_hot, preferred_element_type=jnp.float32
    ).reshape(rows, entry_count * BLK)
    projected = picked[:6]
    colours = picked[6:]
    cotangent = pix_grad.reshape(channels, TPD, -1).astype(jnp.float32)
    picture, grad_proj, grad_colour = tile_grads(projected, colours, cotangent)
    entry_grads = jnp.concatenate([grad_proj, grad_colour], axis=0).astype(jnp.bfloat16)
    back = jnp.einsum(
        "reb,se->rbs",
        entry_grads.reshape(rows, entry_count, BLK),
        slot_hot,
        preferred_element_type=jnp.float32,
    ).astype(jnp.bfloat16)
    returned = lax.all_to_all(back, "tiles", split_axis=2, concat_axis=2, tiled=True)
    summed = jnp.einsum("rbs,ks->rbk", returned, owner_hot, preferred_element_type=jnp.float32)
    column_geometry = project_pullback(geometry_col, linear, summed[:6])
    column_colour = summed[6:]
    column_all = jnp.concatenate([column_geometry, column_colour], axis=0)
    grads = lax.all_to_all(
        column_all.reshape(rows, BLK, cams, local_blocks), "cams", 2, 2, tiled=True
    ).sum(axis=2)
    grads = grads.transpose(0, 2, 1).reshape(rows, local_blocks * BLK)
    grad_geometry = grads[:6]
    grad_appearance = grads[6:]
    return (picture.reshape(channels, 1, -1), grad_geometry, grad_appearance)


def solution(mesh):
    return jax.shard_map(
        local,
        mesh=mesh,
        in_specs=(
            P(None, ("tiles", "cams")),
            P(None, ("tiles", "cams")),
            P(("tiles", "cams")),
            P(("tiles", "cams")),
            P(None, ("tiles", "cams")),
            P("cams", None),
            P("cams", None),
            P("cams", "tiles", None, None),
            P(None, "cams", "tiles"),
        ),
        out_specs=(
            P(None, "cams", "tiles"),
            P(None, ("tiles", "cams")),
            P(None, ("tiles", "cams")),
        ),
        check_vma=False,
    )
```
